256 devices in a mesh: energy: 64 (over z, y, core), atoms: 4 (over x).
Axes of the slice: x: 4, y: 4, z: 8, core: 2. Of those that a mesh axis runs over, the one named last changes fastest.
Arguments:
- green: bfloat16 [1024, 256, 288], P('energy', 'atoms'), may hold values from -6 to 6
- superop: bfloat16 [4, 288, 288], replicated, may hold values from -0.1875 to 0.1875
- phonon: bfloat16 [64, 2048], replicated, may hold values from -0.1875 to 0.1875
- owner: int32 [256, 1], P('atoms'), may hold values from 0 to 63; in each aligned block of 64 rows (0 to 63, 64 to 127, ...) at most 4 rows name the same one
- neighbours: int32 [256, 4], P('atoms'), may hold values from -1 to 255, as said below
Outputs:
- self_energy: bfloat16 [1024, 256, 288], P('energy', 'atoms')
The draws below stay inside these ranges and needn't reach their ends.
Inputs may be any that keep to these rules, and one draw needn't show every extreme that they name: `owner`: within each aligned block of 64 atoms (one atom group) no domain holds more than 4 atoms, and some domain holds exactly 4. `neighbours`: each entry is -1 or the index of an atom at most 8 away from the row's atom; some entry lies exactly 8 above its row's atom, in the next atom group.
All inputs are finite; a program needn't handle non-finite values.
Results may differ from the reference program's by a relative error of at most 0.0049.
Values may be sent and summed in bfloat16 or wider, within the bound.
No kernel may reach another device: no remote copies, remote signals or barrier semaphores. Data moves between devices by JAX's collectives and lax.ppermute only.
A program may use at most 64 MiB of HBM per device.

```python
import math
import jax
import jax.numpy as jnp
import numpy as np
from jax import lax

C = 288
NE = 1024
K = 4
HALO = 8
CAP = 4
DOMAINS = 64
GROUP_ATOMS = 64
NA = 256


def draw_neighbours(key, part):
    key_dist, key_side, key_count = jax.random.split(jax.random.fold_in(key, 11), 3)
    atom_ids = jnp.arange(NA, dtype=jnp.int32)[:, None]
    distance = jax.random.randint(key_dist, (NA, K), 1, HALO + 1)
    sides = jax.random.randint(key_side, (NA, K), 0, 2) * 2 - 1
    target = atom_ids + distance * sides
    counts = jax.random.randint(key_count, (NA, 1), 1, K + 1)
    slot_ids = jnp.arange(K, dtype=jnp.int32)[None, :]
    edge = GROUP_ATOMS - 1
    forced = (atom_ids == edge) & (slot_ids == 0)
    target = jnp.where(forced, edge + HALO, target)
    keeping = (slot_ids < counts) & (target >= 0) & (target < NA)
    return jnp.where(keeping, target, -1).astype(jnp.int32)


def shard_levels(own_key, extent, shards, smallest, top_value):
    level, own = 1.0, jax.random.fold_in(own_key, 6)
    for axis_at, parts in shards:
        steps = jnp.exp(jax.random.uniform(jax.random.fold_in(own, axis_at), (parts,), jnp.float32, smallest / len(shards), top_value / len(shards)))
        level = level * jnp.repeat(steps, extent[axis_at] // parts).reshape([-1 if axis == axis_at else 1 for axis in range(len(extent))])
    return level


def assign_block(stream_key, own, number, rows, number_of, top, most, skew):
    order = jax.random.permutation(stream_key, number_of)
    heavy_load, usual = load_shares(number_of, rows * top, most, skew, True), load_shares(number_of, rows * top, most, skew, False)
    places = jnp.arange(number_of)

    def named(tallies, rotation):
        used = int((tallies > 0).sum())
        fixed = max(1, used // 4)
        shifted = fixed + (places - fixed + rotation * (used - fixed)) % max(1, number_of - fixed)
        return jnp.zeros((number_of,), jnp.int32).at[order[jnp.where(places < fixed, places, shifted)]].set(jnp.asarray(tallies, jnp.int32))

    tallies = jnp.where(number % 4 == 0, named(heavy_load, number // 4), named(usual, number - number // 4 - 1))
    mixed = jax.random.permutation(jax.random.fold_in(own, 3), number_of)
    giver, taker = mixed[0:number_of // 2 * 2:2], mixed[1:number_of // 2 * 2:2]
    slack = jnp.minimum(tallies[giver] - 1, most - tallies[taker]) // 2
    slack = jnp.where((giver == order[0]) | (taker == order[0]) | (tallies[taker] == 0), 0, jnp.maximum(slack, 0))
    shifted = jax.random.randint(jax.random.fold_in(own, 4), (number_of // 2,), 0, 1 << 20) % (slack + 1)
    tallies = tallies.at[giver].add(-shifted).at[taker].add(shifted)
    items = jnp.searchsorted(jnp.cumsum(tallies), jnp.arange(rows * top), side="right").astype(jnp.int32)
    table = items.reshape(top, rows).T
    table = table[jax.random.permutation(jax.random.fold_in(own, 1), rows)]
    rotation = jax.random.randint(jax.random.fold_in(own, 2), (rows, 1), 0, top)
    return jnp.take_along_axis(table, (jnp.arange(top)[None, :] + rotation) % top, axis=1)


def load_shares(count, total, reach, lean, full):
    weights = [(1 << 20) // math.isqrt(rank ** lean) + 1 for rank in range(1, count + 1)]
    largest = reach if full else min(reach, max(-(-total // count), total * weights[0] // sum(weights)))
    least = 1 if total - largest >= count - 1 else 0
    holding, rest = [largest] + [least] * (count - 1), total - largest - least * (count - 1)
    while rest > 0:
        free = [i for i in range(1, count) if holding[i] < largest] or [i for i in range(1, count) if holding[i] < reach]
        whole, remaining = sum([weights[i] for i in free]), rest
        for i in free:
            addition = min(reach - holding[i], max(1, remaining * weights[i] // whole), rest)
            holding[i] = holding[i] + addition
            rest = rest - addition
    return np.array(holding)


def bell_draw(key, shape, spread, limit, cuts=(), kind=jnp.bfloat16):
    level = shard_levels(key, shape, cuts, -0.22, 0.18) if cuts else 1.0
    entries = jax.random.normal(key, shape, jnp.float32) * spread * level
    return jnp.minimum(jnp.maximum(entries, -limit), limit).astype(kind)


def setup_inputs(seed: int = 0) -> dict:
    keys = jax.random.split(jax.random.key(seed), 6)
    green = bell_draw(keys[0], (NE, NA, C), 1.0, 6.0, ((0, 64), (1, 4)))
    superop = bell_draw(keys[1], (K, C, C), (K * C) ** -0.5, 0.1875)
    phonon = bell_draw(keys[2], (DOMAINS, 2 * NE), NE ** -0.5, 0.1875)
    owner_keys = jax.random.split(jax.random.fold_in(keys[3], 1), NA // GROUP_ATOMS)
    owner_turns = jax.random.permutation(jax.random.fold_in(keys[3], 3), NA // GROUP_ATOMS)
    owner = jax.vmap(lambda own, number: assign_block(jax.random.fold_in(keys[3], 2), own, number, GROUP_ATOMS, DOMAINS, 1, CAP, 2))(owner_keys, owner_turns).reshape((NA, 1))
    neighbours = draw_neighbours(jax.random.fold_in(keys[5], 71), 0)
    return {"green": green, "superop": superop, "phonon": phonon, "owner": owner, "neighbours": neighbours}


def toeplitz_rows(kernel_row, count):
    length = 2 * count
    flipped = kernel_row[::-1]
    tiled = jnp.tile(flipped, count)[: count * (length - 1)]
    return tiled.reshape(count, length - 1)[:, count - 1: 2 * count - 1]


def reference(green, superop, phonon, owner, neighbours):
    present = neighbours >= 0
    target_rows = jnp.where(present, neighbours, 0).astype(jnp.int32)
    summed = jnp.zeros((NE * NA, C), jnp.float32)
    for neighbour_slot in range(K):
        gathered = jnp.take(green, target_rows[:, neighbour_slot], axis=1)
        gathered = jnp.where(present[:, neighbour_slot][None, :, None], gathered, jnp.zeros_like(gathered))
        summed = summed + jnp.dot(gathered.reshape(NE * NA, C), superop[neighbour_slot], preferred_element_type=jnp.float32)
    coupled = summed.reshape(NE, NA, C).astype(jnp.bfloat16)
    per_atom = jnp.transpose(coupled, (1, 0, 2))

    def one_atom(pair_args):
        domain, columns = pair_args
        kernel = toeplitz_rows(phonon[domain], NE)
        return jnp.dot(kernel, columns, preferred_element_type=jnp.float32).astype(jnp.bfloat16)

    per_result = lax.map(one_atom, (owner[:, 0], per_atom))
    return jnp.transpose(per_result, (1, 0, 2))
```

```python
import jax
import jax.numpy as jnp
from jax import lax
from jax.experimental import pallas as pl
from jax.experimental.pallas import tpu as pltpu
from jax.sharding import PartitionSpec as P

HALO = 8
ATOMS_DEV = 1


def padded(block, sides, width):
    for axis, dim in sides:
        count = lax.axis_size(axis)
        forward = [(i, i + 1) for i in range(count - 1)]
        backward = [(target, source) for source, target in forward]
        low = lax.ppermute(
            lax.slice_in_dim(block, block.shape[dim] - width, None, axis=dim), axis, forward
        )
        high = lax.ppermute(lax.slice_in_dim(block, 0, width, axis=dim), axis, backward)
        block = jnp.concatenate([low, block, high], axis=dim)
    return block


def toeplitz_kernel(domain_ref, phonon_ref, columns_ref, out_ref):
    count = columns_ref.shape[0]
    row = phonon_ref[0].astype(jnp.float32)
    wide = jnp.broadcast_to(row, (count, 2 * count))
    rolled = pltpu.roll(wide, shift=count + 1, axis=1, stride=1, stride_axis=0)
    kernel = rolled[:, :count].astype(jnp.bfloat16)
    out_ref[...] = jnp.dot(
        kernel, columns_ref[...], preferred_element_type=jnp.float32
    ).astype(out_ref.dtype)


def toeplitz_apply(domain, phonon_rev, columns):
    count, comps = columns.shape
    return pl.pallas_call(
        toeplitz_kernel,
        out_shape=jax.ShapeDtypeStruct((count, comps), jnp.bfloat16),
        grid_spec=pltpu.PrefetchScalarGridSpec(
            num_scalar_prefetch=1,
            grid=(1,),
            in_specs=[
                pl.BlockSpec((1, 1, 2 * count), lambda i, d: (d[0], 0, 0)),
                pl.BlockSpec((count, comps), lambda i, d: (0, 0)),
            ],
            out_specs=pl.BlockSpec((count, comps), lambda i, d: (0, 0)),
        ),
        cost_estimate=pl.CostEstimate(
            flops=2 * count * count * comps,
            bytes_accessed=2 * (2 * count + 2 * count * comps),
            transcendentals=0,
        ),
    )(domain, phonon_rev, columns)


def per_device(green, superop, phonon, owner, neighbours):
    local_energies = green.shape[0]
    group_size = green.shape[1]
    comps = green.shape[2]
    slots = neighbours.shape[1]
    group = lax.axis_index("atoms")
    widened = padded(green, (("atoms", 1),), HALO)
    present = neighbours >= 0
    target_rows = jnp.where(present, neighbours - group * group_size + HALO, 0)
    picked = jnp.take(widened, target_rows.reshape(-1), axis=1)
    picked = jnp.where(present.reshape(1, -1, 1), picked, jnp.zeros_like(picked))
    coupled = jnp.dot(
        picked.reshape(local_energies * group_size, slots * comps),
        superop.reshape(slots * comps, comps),
        preferred_element_type=jnp.float32,
    )
    coupled = coupled.reshape(local_energies, group_size, comps).astype(jnp.bfloat16)
    count = local_energies * lax.axis_size("energy")
    energy_rank = lax.axis_index("energy")
    mine = lax.dynamic_slice_in_dim(owner[:, 0], energy_rank * ATOMS_DEV, ATOMS_DEV)
    phonon_rev = phonon[:, ::-1].reshape(phonon.shape[0], 1, phonon.shape[1])
    columns = lax.all_to_all(coupled, "energy", split_axis=1, concat_axis=0, tiled=True)
    product = toeplitz_apply(mine, phonon_rev, columns.reshape(count, comps))
    result = lax.all_to_all(
        product.reshape(count, ATOMS_DEV, comps), "energy", split_axis=0, concat_axis=1, tiled=True
    )
    return result


def solution(mesh):
    return jax.shard_map(
        per_device,
        mesh=mesh,
        in_specs=(P("energy", "atoms", None), P(), P(), P("atoms", None), P("atoms", None)),
        out_specs=P("energy", "atoms", None),
        check_vma=False,
    )
```

```python
import jax
import jax.numpy as jnp
from jax import lax
from jax.experimental import pallas as pl
from jax.experimental.pallas import tpu as pltpu
from jax.sharding import PartitionSpec as P

HALO = 8
ATOMS_DEV = 1


def padded(block, sides, width):
    for axis, dim in sides:
        count = lax.axis_size(axis)
        forward = [(i, i + 1) for i in range(count - 1)]
        backward = [(target, source) for source, target in forward]
        low = lax.ppermute(
            lax.slice_in_dim(block, block.shape[dim] - width, None, axis=dim), axis, forward
        )
        high = lax.ppermute(lax.slice_in_dim(block, 0, width, axis=dim), axis, backward)
        block = jnp.concatenate([low, block, high], axis=dim)
    return block


def toeplitz_kernel(domain_ref, phonon_ref, columns_ref, out_ref):
    count = columns_ref.shape[0]
    row = phonon_ref[0].astype(jnp.float32)
    wide = jnp.broadcast_to(row, (count, 2 * count))
    rolled = pltpu.roll(wide, shift=count + 1, axis=1, stride=1, stride_axis=0)
    kernel = rolled[:, :count].astype(jnp.bfloat16)
    out_ref[...] = jnp.dot(
        kernel, columns_ref[...], preferred_element_type=jnp.float32
    ).astype(out_ref.dtype)


def toeplitz_apply(domain, phonon_rev, columns):
    count, comps = columns.shape
    return pl.pallas_call(
        toeplitz_kernel,
        out_shape=jax.ShapeDtypeStruct((count, comps), jnp.bfloat16),
        grid_spec=pltpu.PrefetchScalarGridSpec(
            num_scalar_prefetch=1,
            grid=(1,),
            in_specs=[
                pl.BlockSpec((1, 1, 2 * count), lambda i, d: (d[0], 0, 0)),
                pl.BlockSpec((count, comps), lambda i, d: (0, 0)),
            ],
            out_specs=pl.BlockSpec((count, comps), lambda i, d: (0, 0)),
        ),
        cost_estimate=pl.CostEstimate(
            flops=2 * count * count * comps,
            bytes_accessed=2 * (2 * count + 2 * count * comps),
            transcendentals=0,
        ),
    )(domain, phonon_rev, columns)


def neighbour_kernel(select_ref, widened_ref, superop_ref, out_ref):
    energies, rows, comps = widened_ref.shape
    atoms = select_ref.shape[1]
    widened = widened_ref[...]
    total = jnp.zeros((energies * atoms, comps), jnp.float32)
    for slot in range(select_ref.shape[0]):
        select = jnp.broadcast_to(select_ref[slot], (energies, atoms, rows))
        picked = lax.dot_general(
            select, widened, (((2,), (1,)), ((0,), (0,))), preferred_element_type=jnp.float32
        )
        picked = picked.astype(jnp.bfloat16).reshape(energies * atoms, comps)
        total = total + jnp.dot(picked, superop_ref[slot], preferred_element_type=jnp.float32)
    out_ref[...] = total.astype(out_ref.dtype).reshape(energies, atoms, comps)


def neighbour_apply(select, widened, superop):
    energies, rows, comps = widened.shape
    slots, atoms, _ = select.shape
    vmem = pl.BlockSpec(memory_space=pltpu.VMEM)
    return pl.pallas_call(
        neighbour_kernel,
        out_shape=jax.ShapeDtypeStruct((energies, atoms, comps), jnp.bfloat16),
        in_specs=[vmem, vmem, vmem],
        out_specs=vmem,
        cost_estimate=pl.CostEstimate(
            flops=2 * slots * energies * atoms * comps * (rows + comps),
            bytes_accessed=2 * (widened.size + superop.size + select.size + energies * atoms * comps),
            transcendentals=0,
        ),
    )(select, widened, superop)


def per_device(green, superop, phonon, owner, neighbours):
    local_energies = green.shape[0]
    group_size = green.shape[1]
    comps = green.shape[2]
    group = lax.axis_index("atoms")
    widened = padded(green, (("atoms", 1),), HALO)
    present = neighbours >= 0
    target_rows = jnp.where(present, neighbours - group * group_size + HALO, -1)
    rows = jnp.arange(widened.shape[1], dtype=jnp.int32)
    select = (target_rows.T[:, :, None] == rows[None, None, :]).astype(jnp.bfloat16)
    coupled = neighbour_apply(select, widened, superop)
    count = local_energies * lax.axis_size("energy")
    energy_rank = lax.axis_index("energy")
    mine = lax.dynamic_slice_in_dim(owner[:, 0], energy_rank * ATOMS_DEV, ATOMS_DEV)
    phonon_rev = phonon[:, ::-1].reshape(phonon.shape[0], 1, phonon.shape[1])
    columns = lax.all_to_all(coupled, "energy", split_axis=1, concat_axis=0, tiled=True)
    product = toeplitz_apply(mine, phonon_rev, columns.reshape(count, comps))
    result = lax.all_to_all(
        product.reshape(count, ATOMS_DEV, comps), "energy", split_axis=0, concat_axis=1, tiled=True
    )
    return result


def solution(mesh):
    return jax.shard_map(
        per_device,
        mesh=mesh,
        in_specs=(P("energy", "atoms", None), P(), P(), P("atoms", None), P("atoms", None)),
        out_specs=P("energy", "atoms", None),
        check_vma=False,
    )
```

```python
import jax
import jax.numpy as jnp
from jax import lax
from jax.experimental import pallas as pl
from jax.experimental.pallas import tpu as pltpu
from jax.sharding import PartitionSpec as P

HALO = 8
ATOMS_DEV = 1


def padded(block, sides, width):
    for axis, dim in sides:
        count = lax.axis_size(axis)
        forward = [(i, i + 1) for i in range(count - 1)]
        backward = [(target, source) for source, target in forward]
        low = lax.ppermute(
            lax.slice_in_dim(block, block.shape[dim] - width, None, axis=dim), axis, forward
        )
        high = lax.ppermute(lax.slice_in_dim(block, 0, width, axis=dim), axis, backward)
        block = jnp.concatenate([low, block, high], axis=dim)
    return block


def toeplitz_kernel(owner_ref, phonon_ref, columns_ref, out_ref):
    count = columns_ref.shape[0]
    domain = owner_ref[lax.axis_index("energy"), 0]
    base = pl.multiple_of((domain // 16) * 16, 16)
    block = phonon_ref[pl.ds(base, 16), :].astype(jnp.float32)
    rows = lax.broadcasted_iota(jnp.int32, block.shape, 0)
    row = jnp.sum(jnp.where(rows == domain - base, block, 0.0), axis=0, keepdims=True)
    wide = jnp.broadcast_to(row, (count, 2 * count))
    rolled = pltpu.roll(wide, shift=count, axis=1, stride=1, stride_axis=0)
    kernel_t = rolled[:, :count].astype(jnp.bfloat16)
    out_ref[...] = lax.dot_general(
        kernel_t, columns_ref[...], (((0,), (0,)), ((), ())), preferred_element_type=jnp.float32
    ).astype(out_ref.dtype)


def toeplitz_apply(owner, phonon, columns):
    count, comps = columns.shape
    vmem = pl.BlockSpec(memory_space=pltpu.VMEM)
    return pl.pallas_call(
        toeplitz_kernel,
        out_shape=jax.ShapeDtypeStruct((count, comps), jnp.bfloat16),
        in_specs=[pl.BlockSpec(memory_space=pltpu.SMEM), vmem, vmem],
        out_specs=vmem,
        cost_estimate=pl.CostEstimate(
            flops=2 * count * count * comps,
            bytes_accessed=2 * (phonon.size + 2 * count * comps),
            transcendentals=0,
        ),
    )(owner, phonon, columns)


def neighbour_kernel(select_ref, widened_ref, superop_ref, out_ref):
    energies, rows, comps = widened_ref.shape
    atoms = select_ref.shape[1]
    widened = widened_ref[...]
    total = jnp.zeros((energies * atoms, comps), jnp.float32)
    for slot in range(select_ref.shape[0]):
        select = jnp.broadcast_to(select_ref[slot], (energies, atoms, rows))
        picked = lax.dot_general(
            select, widened, (((2,), (1,)), ((0,), (0,))), preferred_element_type=jnp.float32
        )
        picked = picked.astype(jnp.bfloat16).reshape(energies * atoms, comps)
        total = total + jnp.dot(picked, superop_ref[slot], preferred_element_type=jnp.float32)
    out_ref[...] = total.astype(out_ref.dtype).reshape(energies, atoms, comps)


def neighbour_apply(select, widened, superop):
    energies, rows, comps = widened.shape
    slots, atoms, _ = select.shape
    vmem = pl.BlockSpec(memory_space=pltpu.VMEM)
    return pl.pallas_call(
        neighbour_kernel,
        out_shape=jax.ShapeDtypeStruct((energies, atoms, comps), jnp.bfloat16),
        in_specs=[vmem, vmem, vmem],
        out_specs=vmem,
        cost_estimate=pl.CostEstimate(
            flops=2 * slots * energies * atoms * comps * (rows + comps),
            bytes_accessed=2 * (widened.size + superop.size + select.size + energies * atoms * comps),
            transcendentals=0,
        ),
    )(select, widened, superop)


def per_device(green, superop, phonon, owner, neighbours):
    local_energies = green.shape[0]
    group_size = green.shape[1]
    comps = green.shape[2]
    group = lax.axis_index("atoms")
    widened = padded(green, (("atoms", 1),), HALO)
    present = neighbours >= 0
    target_rows = jnp.where(present, neighbours - group * group_size + HALO, -1)
    rows = jnp.arange(widened.shape[1], dtype=jnp.int32)
    select = (target_rows.T[:, :, None] == rows[None, None, :]).astype(jnp.bfloat16)
    coupled = neighbour_apply(select, widened, superop)
    count = local_energies * lax.axis_size("energy")
    columns = lax.all_to_all(coupled, "energy", split_axis=1, concat_axis=0, tiled=True)
    product = toeplitz_apply(owner, phonon, columns.reshape(count, comps))
    result = lax.all_to_all(
        product.reshape(count, ATOMS_DEV, comps), "energy", split_axis=0, concat_axis=1, tiled=True
    )
    return result


def solution(mesh):
    return jax.shard_map(
        per_device,
        mesh=mesh,
        in_specs=(P("energy", "atoms", None), P(), P(), P("atoms", None), P("atoms", None)),
        out_specs=P("energy", "atoms", None),
        check_vma=False,
    )
```

```python
import jax
import jax.numpy as jnp
from jax import lax
from jax.experimental import pallas as pl
from jax.experimental.pallas import tpu as pltpu
from jax.sharding import PartitionSpec as P

HALO = 8
ATOMS_DEV = 1


def padded(block, sides, width):
    for axis, dim in sides:
        count = lax.axis_size(axis)
        forward = [(i, i + 1) for i in range(count - 1)]
        backward = [(target, source) for source, target in forward]
        low = lax.ppermute(
            lax.slice_in_dim(block, block.shape[dim] - width, None, axis=dim), axis, forward
        )
        high = lax.ppermute(lax.slice_in_dim(block, 0, width, axis=dim), axis, backward)
        block = jnp.concatenate([low, block, high], axis=dim)
    return block


def toeplitz_kernel(owner_ref, phonon_ref, columns_ref, out_ref):
    count = columns_ref.shape[0]
    domain = owner_ref[lax.axis_index("energy"), 0]
    base = pl.multiple_of((domain // 16) * 16, 16)
    block = phonon_ref[pl.ds(base, 16), :].astype(jnp.float32)
    rows = lax.broadcasted_iota(jnp.int32, block.shape, 0)
    row = jnp.sum(jnp.where(rows == domain - base, block, 0.0), axis=0, keepdims=True)
    wide = jnp.broadcast_to(row, (count, 2 * count))
    rolled = pltpu.roll(wide, shift=count, axis=1, stride=1, stride_axis=0)
    kernel_t = rolled[:, :count].astype(jnp.bfloat16)
    out_ref[...] = lax.dot_general(
        kernel_t, columns_ref[...], (((0,), (0,)), ((), ())), preferred_element_type=jnp.float32
    ).astype(out_ref.dtype)


def toeplitz_apply(owner, phonon, columns):
    count, comps = columns.shape
    vmem = pl.BlockSpec(memory_space=pltpu.VMEM)
    return pl.pallas_call(
        toeplitz_kernel,
        out_shape=jax.ShapeDtypeStruct((count, comps), jnp.bfloat16),
        in_specs=[pl.BlockSpec(memory_space=pltpu.SMEM), vmem, vmem],
        out_specs=vmem,
        cost_estimate=pl.CostEstimate(
            flops=2 * count * count * comps,
            bytes_accessed=2 * (phonon.size + 2 * count * comps),
            transcendentals=0,
        ),
    )(owner, phonon, columns)


def neighbour_kernel(select_ref, widened_ref, superop_ref, out_ref):
    energies, rows, comps = widened_ref.shape
    atoms = select_ref.shape[1]
    widened = widened_ref[...]
    total = jnp.zeros((energies * atoms, comps), jnp.float32)
    for slot in range(select_ref.shape[0]):
        select = jnp.broadcast_to(select_ref[slot], (energies, atoms, rows))
        picked = lax.dot_general(
            select, widened, (((2,), (1,)), ((0,), (0,))), preferred_element_type=jnp.float32
        )
        picked = picked.astype(jnp.bfloat16).reshape(energies * atoms, comps)
        total = total + jnp.dot(picked, superop_ref[slot], preferred_element_type=jnp.float32)
    out_ref[...] = total.astype(out_ref.dtype).reshape(energies, atoms, comps)


def neighbour_apply(select, widened, superop):
    energies, rows, comps = widened.shape
    slots, atoms, _ = select.shape
    vmem = pl.BlockSpec(memory_space=pltpu.VMEM)
    return pl.pallas_call(
        neighbour_kernel,
        out_shape=jax.ShapeDtypeStruct((energies, atoms, comps), jnp.bfloat16),
        in_specs=[vmem, vmem, vmem],
        out_specs=vmem,
        cost_estimate=pl.CostEstimate(
            flops=2 * slots * energies * atoms * comps * (rows + comps),
            bytes_accessed=2 * (widened.size + superop.size + select.size + energies * atoms * comps),
            transcendentals=0,
        ),
    )(select, widened, superop)


def per_device(green, superop, phonon, owner, neighbours):
    local_energies = green.shape[0]
    group_size = green.shape[1]
    comps = green.shape[2]
    group = lax.axis_index("atoms")
    widened = padded(green, (("atoms", 1),), HALO)
    present = neighbours >= 0
    target_rows = jnp.where(present, neighbours - group * group_size + HALO, -1)
    rows = jnp.arange(widened.shape[1], dtype=jnp.int32)
    select = (target_rows.T[:, :, None] == rows[None, None, :]).astype(jnp.bfloat16)
    coupled = neighbour_apply(select, widened, superop)
    count = local_energies * lax.axis_size("energy")
    peers = lax.axis_size("energy")
    outgoing = jnp.transpose(coupled, (1, 0, 2)).reshape(peers, 2, local_energies * comps // 2)
    columns = lax.all_to_all(outgoing, "energy", split_axis=0, concat_axis=0, tiled=True)
    product = toeplitz_apply(owner, phonon, columns.reshape(count, comps))
    result = lax.all_to_all(
        product.reshape(count, ATOMS_DEV, comps), "energy", split_axis=0, concat_axis=1, tiled=True
    )
    return result


def solution(mesh):
    return jax.shard_map(
        per_device,
        mesh=mesh,
        in_specs=(P("energy", "atoms", None), P(), P(), P("atoms", None), P("atoms", None)),
        out_specs=P("energy", "atoms", None),
        check_vma=False,
    )
```

```python
import jax
import jax.numpy as jnp
from jax import lax
from jax.experimental import pallas as pl
from jax.experimental.pallas import tpu as pltpu
from jax.sharding import PartitionSpec as P

HALO = 8
ATOMS_DEV = 1


def padded(block, sides, width):
    for axis, dim in sides:
        count = lax.axis_size(axis)
        forward = [(i, i + 1) for i in range(count - 1)]
        backward = [(target, source) for source, target in forward]
        low = lax.ppermute(
            lax.slice_in_dim(block, block.shape[dim] - width, None, axis=dim), axis, forward
        )
        high = lax.ppermute(lax.slice_in_dim(block, 0, width, axis=dim), axis, backward)
        block = jnp.concatenate([low, block, high], axis=dim)
    return block


def toeplitz_kernel(owner_ref, phonon_ref, columns_ref, out_ref):
    count = columns_ref.shape[0]
    domain = owner_ref[0]
    base = pl.multiple_of((domain // 16) * 16, 16)
    block = phonon_ref[pl.ds(base, 16), :].astype(jnp.float32)
    rows = lax.broadcasted_iota(jnp.int32, block.shape, 0)
    row = jnp.sum(jnp.where(rows == domain - base, block, 0.0), axis=0, keepdims=True)
    wide = jnp.broadcast_to(row, (count, 2 * count))
    rolled = pltpu.roll(wide, shift=count, axis=1, stride=1, stride_axis=0)
    kernel_t = rolled[:, :count].astype(jnp.bfloat16)
    out_ref[...] = lax.dot_general(
        kernel_t, columns_ref[...], (((0,), (0,)), ((), ())), preferred_element_type=jnp.float32
    ).astype(out_ref.dtype)


def toeplitz_apply(owner, phonon, columns):
    count, comps = columns.shape
    vmem = pl.BlockSpec(memory_space=pltpu.VMEM)
    return pl.pallas_call(
        toeplitz_kernel,
        out_shape=jax.ShapeDtypeStruct((count, comps), jnp.bfloat16),
        in_specs=[pl.BlockSpec(memory_space=pltpu.SMEM), vmem, vmem],
        out_specs=vmem,
        cost_estimate=pl.CostEstimate(
            flops=2 * count * count * comps,
            bytes_accessed=2 * (phonon.size + 2 * count * comps),
            transcendentals=0,
        ),
    )(owner, phonon, columns)


def neighbour_kernel(select_ref, widened_ref, superop_ref, out_ref):
    energies, rows, comps = widened_ref.shape
    atoms = select_ref.shape[1]
    widened = widened_ref[...]
    total = jnp.zeros((energies * atoms, comps), jnp.float32)
    for slot in range(select_ref.shape[0]):
        select = jnp.broadcast_to(select_ref[slot], (energies, atoms, rows))
        picked = lax.dot_general(
            select, widened, (((2,), (1,)), ((0,), (0,))), preferred_element_type=jnp.float32
        )
        picked = picked.astype(jnp.bfloat16).reshape(energies * atoms, comps)
        total = total + jnp.dot(picked, superop_ref[slot], preferred_element_type=jnp.float32)
    out_ref[...] = total.astype(out_ref.dtype).reshape(energies, atoms, comps)


def neighbour_apply(select, widened, superop):
    energies, rows, comps = widened.shape
    slots, atoms, _ = select.shape
    vmem = pl.BlockSpec(memory_space=pltpu.VMEM)
    return pl.pallas_call(
        neighbour_kernel,
        out_shape=jax.ShapeDtypeStruct((energies, atoms, comps), jnp.bfloat16),
        in_specs=[vmem, vmem, vmem],
        out_specs=vmem,
        cost_estimate=pl.CostEstimate(
            flops=2 * slots * energies * atoms * comps * (rows + comps),
            bytes_accessed=2 * (widened.size + superop.size + select.size + energies * atoms * comps),
            transcendentals=0,
        ),
    )(select, widened, superop)


def per_device(green, superop, phonon, owner, neighbours):
    local_energies = green.shape[0]
    group_size = green.shape[1]
    comps = green.shape[2]
    group = lax.axis_index("atoms")
    widened = padded(green, (("atoms", 1),), HALO)
    present = neighbours >= 0
    target_rows = jnp.where(present, neighbours - group * group_size + HALO, -1)
    rows = jnp.arange(widened.shape[1], dtype=jnp.int32)
    select = (target_rows.T[:, :, None] == rows[None, None, :]).astype(jnp.bfloat16)
    coupled = neighbour_apply(select, widened, superop)
    count = local_energies * lax.axis_size("energy")
    peers = lax.axis_size("energy")
    outgoing = jnp.transpose(coupled, (1, 0, 2)).reshape(peers, 2, local_energies * comps // 2)
    mine = lax.dynamic_slice_in_dim(owner[:, 0], lax.axis_index("energy"), 1)
    mine, outgoing = lax.optimization_barrier((mine, outgoing))
    columns = lax.all_to_all(outgoing, "energy", split_axis=0, concat_axis=0, tiled=True)
    product = toeplitz_apply(mine, phonon, columns.reshape(count, comps))
    result = lax.all_to_all(
        product.reshape(count, ATOMS_DEV, comps), "energy", split_axis=0, concat_axis=1, tiled=True
    )
    return result


def solution(mesh):
    return jax.shard_map(
        per_device,
        mesh=mesh,
        in_specs=(P("energy", "atoms", None), P(), P(), P("atoms", None), P("atoms", None)),
        out_specs=P("energy", "atoms", None),
        check_vma=False,
    )
```

```python
import jax
import jax.numpy as jnp
from jax import lax
from jax.experimental import pallas as pl
from jax.experimental.pallas import tpu as pltpu
from jax.sharding import PartitionSpec as P

HALO = 8
EDGE = 16
ATOMS_DEV = 1


def toeplitz_kernel(owner_ref, phonon_ref, columns_ref, out_ref):
    count = columns_ref.shape[0]
    domain = owner_ref[0]
    base = pl.multiple_of((domain // 16) * 16, 16)
    block = phonon_ref[pl.ds(base, 16), :].astype(jnp.float32)
    rows = lax.broadcasted_iota(jnp.int32, block.shape, 0)
    row = jnp.sum(jnp.where(rows == domain - base, block, 0.0), axis=0, keepdims=True)
    wide = jnp.broadcast_to(row, (count, 2 * count))
    rolled = pltpu.roll(wide, shift=count, axis=1, stride=1, stride_axis=0)
    kernel_t = rolled[:, :count].astype(jnp.bfloat16)
    out_ref[...] = lax.dot_general(
        kernel_t, columns_ref[...], (((0,), (0,)), ((), ())), preferred_element_type=jnp.float32
    ).astype(out_ref.dtype)


def toeplitz_apply(owner, phonon, columns):
    count, comps = columns.shape
    vmem = pl.BlockSpec(memory_space=pltpu.VMEM)
    return pl.pallas_call(
        toeplitz_kernel,
        out_shape=jax.ShapeDtypeStruct((count, comps), jnp.bfloat16),
        in_specs=[pl.BlockSpec(memory_space=pltpu.SMEM), vmem, vmem],
        out_specs=vmem,
        cost_estimate=pl.CostEstimate(
            flops=2 * count * count * comps,
            bytes_accessed=2 * (phonon.size + 2 * count * comps),
            transcendentals=0,
        ),
    )(owner, phonon, columns)


def couple_rows(select_refs, source_refs, superop_ref):
    energies, _, comps = source_refs[0].shape
    atoms = select_refs[0].shape[1]
    sources = [ref[...] for ref in source_refs]
    total = jnp.zeros((energies * atoms, comps), jnp.float32)
    for slot in range(select_refs[0].shape[0]):
        picked = jnp.zeros((energies, atoms, comps), jnp.float32)
        for select_ref, source in zip(select_refs, sources):
            select = jnp.broadcast_to(select_ref[slot], (energies, atoms, source.shape[1]))
            picked = picked + lax.dot_general(
                select, source, (((2,), (1,)), ((0,), (0,))), preferred_element_type=jnp.float32
            )
        picked = picked.astype(jnp.bfloat16).reshape(energies * atoms, comps)
        total = total + jnp.dot(picked, superop_ref[slot], preferred_element_type=jnp.float32)
    return total.astype(jnp.bfloat16).reshape(energies, atoms, comps)


def interior_kernel(select_ref, green_ref, superop_ref, out_ref):
    out_ref[...] = couple_rows([select_ref], [green_ref], superop_ref)


def edge_kernel(low_sel, mid_sel, high_sel, low_ref, green_ref, high_ref, superop_ref, base_ref, out_ref):
    edges = couple_rows([low_sel, mid_sel, high_sel], [low_ref, green_ref, high_ref], superop_ref)
    width = low_ref.shape[1]
    atoms = out_ref.shape[1]
    out_ref[...] = base_ref[...]
    out_ref[:, :width, :] = edges[:, :width, :]
    out_ref[:, atoms - width:, :] = edges[:, width:, :]


def couple_call(kernel, args, out_shape, flops):
    vmem = pl.BlockSpec(memory_space=pltpu.VMEM)
    return pl.pallas_call(
        kernel,
        out_shape=jax.ShapeDtypeStruct(out_shape, jnp.bfloat16),
        in_specs=[vmem] * len(args),
        out_specs=vmem,
        cost_estimate=pl.CostEstimate(
            flops=flops,
            bytes_accessed=sum(2 * a.size for a in args) + 2 * out_shape[0] * out_shape[1] * out_shape[2],
            transcendentals=0,
        ),
    )(*args)


def per_device(green, superop, phonon, owner, neighbours):
    local_energies = green.shape[0]
    group_size = green.shape[1]
    comps = green.shape[2]
    slots = neighbours.shape[1]
    group = lax.axis_index("atoms")
    groups = lax.axis_size("atoms")
    forward = [(i, i + 1) for i in range(groups - 1)]
    backward = [(i + 1, i) for i in range(groups - 1)]
    low = lax.ppermute(green[:, group_size - EDGE:, :], "atoms", forward)
    high = lax.ppermute(green[:, :EDGE, :], "atoms", backward)
    present = neighbours >= 0
    target = jnp.where(present, neighbours - group * group_size, -4 * group_size).T
    mid_rows = jnp.arange(group_size, dtype=jnp.int32)
    edge_rows = jnp.arange(EDGE, dtype=jnp.int32)
    select_mid = (target[:, :, None] == mid_rows).astype(jnp.bfloat16)
    edge_target = jnp.concatenate([target[:, :EDGE], target[:, group_size - EDGE:]], axis=1)
    select_low = (edge_target[:, :, None] == edge_rows - EDGE).astype(jnp.bfloat16)
    select_edge = (edge_target[:, :, None] == mid_rows).astype(jnp.bfloat16)
    select_high = (edge_target[:, :, None] == edge_rows + group_size).astype(jnp.bfloat16)
    shape = (local_energies, group_size, comps)
    base = couple_call(
        interior_kernel, (select_mid, green, superop), shape,
        2 * slots * local_energies * group_size * comps * (group_size + comps),
    )
    coupled = couple_call(
        edge_kernel,
        (select_low, select_edge, select_high, low, green, high, superop, base), shape,
        2 * slots * local_energies * 2 * EDGE * comps * (group_size + 2 * EDGE + comps),
    )
    count = local_energies * lax.axis_size("energy")
    peers = lax.axis_size("energy")
    outgoing = jnp.transpose(coupled, (1, 0, 2)).reshape(peers, 2, local_energies * comps // 2)
    mine = lax.dynamic_slice_in_dim(owner[:, 0], lax.axis_index("energy"), 1)
    mine, outgoing = lax.optimization_barrier((mine, outgoing))
    columns = lax.all_to_all(outgoing, "energy", split_axis=0, concat_axis=0, tiled=True)
    product = toeplitz_apply(mine, phonon, columns.reshape(count, comps))
    result = lax.all_to_all(
        product.reshape(count, ATOMS_DEV, comps), "energy", split_axis=0, concat_axis=1, tiled=True
    )
    return result


def solution(mesh):
    return jax.shard_map(
        per_device,
        mesh=mesh,
        in_specs=(P("energy", "atoms", None), P(), P(), P("atoms", None), P("atoms", None)),
        out_specs=P("energy", "atoms", None),
        check_vma=False,
    )
```

```python
import jax
import jax.numpy as jnp
from jax import lax
from jax.experimental import pallas as pl
from jax.experimental.pallas import tpu as pltpu
from jax.sharding import PartitionSpec as P

HALO = 8
EDGE = 16
ATOMS_DEV = 1


def toeplitz_kernel(owner_ref, phonon_ref, columns_ref, out_ref):
    count = columns_ref.shape[0]
    domain = owner_ref[0]
    base = pl.multiple_of((domain // 16) * 16, 16)
    block = phonon_ref[pl.ds(base, 16), :].astype(jnp.float32)
    rows = lax.broadcasted_iota(jnp.int32, block.shape, 0)
    row = jnp.sum(jnp.where(rows == domain - base, block, 0.0), axis=0, keepdims=True)
    wide = jnp.broadcast_to(row, (count, 2 * count))
    rolled = pltpu.roll(wide, shift=count, axis=1, stride=1, stride_axis=0)
    kernel_t = rolled[:, :count].astype(jnp.bfloat16)
    out_ref[...] = lax.dot_general(
        kernel_t, columns_ref[...], (((0,), (0,)), ((), ())), preferred_element_type=jnp.float32
    ).astype(out_ref.dtype)


def toeplitz_apply(owner, phonon, columns):
    count, comps = columns.shape
    vmem = pl.BlockSpec(memory_space=pltpu.VMEM)
    return pl.pallas_call(
        toeplitz_kernel,
        out_shape=jax.ShapeDtypeStruct((count, comps), jnp.bfloat16),
        in_specs=[pl.BlockSpec(memory_space=pltpu.SMEM), vmem, vmem],
        out_specs=vmem,
        cost_estimate=pl.CostEstimate(
            flops=2 * count * count * comps,
            bytes_accessed=2 * (phonon.size + 2 * count * comps),
            transcendentals=0,
        ),
    )(owner, phonon, columns)


def neighbour_kernel(index_ref, low_ref, green_ref, high_ref, superop_ref, out_ref, rows_ref, picked_ref):
    width = low_ref.shape[0]
    atoms, energies, comps = green_ref.shape
    slots = superop_ref.shape[0]
    rows_ref[:width] = low_ref[...]
    rows_ref[width:width + atoms] = green_ref[...]
    rows_ref[width + atoms:2 * width + atoms] = high_ref[...]
    rows_ref[2 * width + atoms] = jnp.zeros((energies, comps), rows_ref.dtype)

    def pick(atom, carry):
        for slot in range(slots):
            picked_ref[slot, atom] = rows_ref[index_ref[atom * slots + slot]]
        return carry

    lax.fori_loop(0, atoms, pick, 0, unroll=8)
    total = jnp.zeros((atoms * energies, comps), jnp.float32)
    for slot in range(slots):
        total = total + jnp.dot(
            picked_ref[slot].reshape(atoms * energies, comps),
            superop_ref[slot],
            preferred_element_type=jnp.float32,
        )
    out_ref[...] = total.astype(out_ref.dtype).reshape(atoms, energies, comps)


def neighbour_apply(index, low, green_t, high, superop):
    width = low.shape[0]
    atoms, energies, comps = green_t.shape
    slots = superop.shape[0]
    vmem = pl.BlockSpec(memory_space=pltpu.VMEM)
    return pl.pallas_call(
        neighbour_kernel,
        out_shape=jax.ShapeDtypeStruct(green_t.shape, jnp.bfloat16),
        in_specs=[pl.BlockSpec(memory_space=pltpu.SMEM)] + [vmem] * 4,
        out_specs=vmem,
        scratch_shapes=[
            pltpu.VMEM((2 * width + atoms + 1, energies, comps), jnp.bfloat16),
            pltpu.VMEM((slots, atoms, energies, comps), jnp.bfloat16),
        ],
        cost_estimate=pl.CostEstimate(
            flops=2 * slots * atoms * energies * comps * comps,
            bytes_accessed=2 * (2 * low.size + 2 * green_t.size + superop.size),
            transcendentals=0,
        ),
    )(index, low, green_t, high, superop)


def per_device(green, superop, phonon, owner, neighbours):
    local_energies = green.shape[0]
    group_size = green.shape[1]
    comps = green.shape[2]
    group = lax.axis_index("atoms")
    groups = lax.axis_size("atoms")
    green_t = jnp.transpose(green, (1, 0, 2))
    forward = [(i, i + 1) for i in range(groups - 1)]
    backward = [(i + 1, i) for i in range(groups - 1)]
    low = lax.ppermute(green_t[group_size - EDGE:], "atoms", forward)
    high = lax.ppermute(green_t[:EDGE], "atoms", backward)
    present = neighbours >= 0
    index = jnp.where(present, neighbours - group * group_size + EDGE, 2 * EDGE + group_size)
    coupled = neighbour_apply(index.reshape(-1), low, green_t, high, superop)
    count = local_energies * lax.axis_size("energy")
    peers = lax.axis_size("energy")
    outgoing = coupled.reshape(peers, 2, local_energies * comps // 2)
    mine = lax.dynamic_slice_in_dim(owner[:, 0], lax.axis_index("energy"), 1)
    mine, outgoing = lax.optimization_barrier((mine, outgoing))
    columns = lax.all_to_all(outgoing, "energy", split_axis=0, concat_axis=0, tiled=True)
    product = toeplitz_apply(mine, phonon, columns.reshape(count, comps))
    result = lax.all_to_all(
        product.reshape(count, ATOMS_DEV, comps), "energy", split_axis=0, concat_axis=1, tiled=True
    )
    return result


def solution(mesh):
    return jax.shard_map(
        per_device,
        mesh=mesh,
        in_specs=(P("energy", "atoms", None), P(), P(), P("atoms", None), P("atoms", None)),
        out_specs=P("energy", "atoms", None),
        check_vma=False,
    )
```

```python
import jax
import jax.numpy as jnp
from jax import lax
from jax.experimental import pallas as pl
from jax.experimental.pallas import tpu as pltpu
from jax.sharding import PartitionSpec as P

HALO = 8
EDGE = 8
ATOMS_DEV = 1


def toeplitz_kernel(owner_ref, phonon_ref, columns_ref, out_ref):
    count = columns_ref.shape[0]
    domain = owner_ref[0]
    base = pl.multiple_of((domain // 16) * 16, 16)
    block = phonon_ref[pl.ds(base, 16), :].astype(jnp.float32)
    rows = lax.broadcasted_iota(jnp.int32, block.shape, 0)
    row = jnp.sum(jnp.where(rows == domain - base, block, 0.0), axis=0, keepdims=True)
    wide = jnp.broadcast_to(row, (count, 2 * count))
    rolled = pltpu.roll(wide, shift=count, axis=1, stride=1, stride_axis=0)
    kernel_t = rolled[:, :count].astype(jnp.bfloat16)
    out_ref[...] = lax.dot_general(
        kernel_t, columns_ref[...], (((0,), (0,)), ((), ())), preferred_element_type=jnp.float32
    ).astype(out_ref.dtype)


def toeplitz_apply(owner, phonon, columns):
    count, comps = columns.shape
    vmem = pl.BlockSpec(memory_space=pltpu.VMEM)
    return pl.pallas_call(
        toeplitz_kernel,
        out_shape=jax.ShapeDtypeStruct((count, comps), jnp.bfloat16),
        in_specs=[pl.BlockSpec(memory_space=pltpu.SMEM), vmem, vmem],
        out_specs=vmem,
        cost_estimate=pl.CostEstimate(
            flops=2 * count * count * comps,
            bytes_accessed=2 * (phonon.size + 2 * count * comps),
            transcendentals=0,
        ),
    )(owner, phonon, columns)


def neighbour_kernel(neighbours_ref, low_ref, green_ref, high_ref, superop_ref, out_ref, rows_ref, picked_ref):
    width = low_ref.shape[0]
    atoms, energies, comps = green_ref.shape
    slots = superop_ref.shape[0]
    first = lax.axis_index("atoms") * atoms - width
    empty = 2 * width + atoms
    rows_ref[:width] = low_ref[...]
    rows_ref[width:width + atoms] = green_ref[...]
    rows_ref[width + atoms:2 * width + atoms] = high_ref[...]
    rows_ref[2 * width + atoms] = jnp.zeros((energies, comps), rows_ref.dtype)

    def pick(atom, carry):
        for slot in range(slots):
            target = neighbours_ref[atom, slot]
            row = jnp.where(target >= 0, target - first, empty)
            picked_ref[slot, atom] = rows_ref[row]
        return carry

    lax.fori_loop(0, atoms, pick, 0, unroll=8)
    total = jnp.zeros((atoms * energies, comps), jnp.float32)
    for slot in range(slots):
        total = total + jnp.dot(
            picked_ref[slot].reshape(atoms * energies, comps),
            superop_ref[slot],
            preferred_element_type=jnp.float32,
        )
    out_ref[...] = total.astype(out_ref.dtype).reshape(atoms, energies, comps)


def neighbour_apply(neighbours, low, green_t, high, superop):
    width = low.shape[0]
    atoms, energies, comps = green_t.shape
    slots = superop.shape[0]
    vmem = pl.BlockSpec(memory_space=pltpu.VMEM)
    return pl.pallas_call(
        neighbour_kernel,
        out_shape=jax.ShapeDtypeStruct(green_t.shape, jnp.bfloat16),
        in_specs=[pl.BlockSpec(memory_space=pltpu.SMEM)] + [vmem] * 4,
        out_specs=vmem,
        scratch_shapes=[
            pltpu.VMEM((2 * width + atoms + 1, energies, comps), jnp.bfloat16),
            pltpu.VMEM((slots, atoms, energies, comps), jnp.bfloat16),
        ],
        cost_estimate=pl.CostEstimate(
            flops=2 * slots * atoms * energies * comps * comps,
            bytes_accessed=2 * (2 * low.size + 2 * green_t.size + superop.size),
            transcendentals=0,
        ),
    )(neighbours, low, green_t, high, superop)


def per_device(green, superop, phonon, owner, neighbours):
    local_energies = green.shape[0]
    group_size = green.shape[1]
    comps = green.shape[2]
    groups = lax.axis_size("atoms")
    green_t = jnp.transpose(green, (1, 0, 2))
    forward = [(i, i + 1) for i in range(groups - 1)]
    backward = [(i + 1, i) for i in range(groups - 1)]
    low = lax.ppermute(green_t[group_size - EDGE:], "atoms", forward)
    high = lax.ppermute(green_t[:EDGE], "atoms", backward)
    coupled = neighbour_apply(neighbours, low, green_t, high, superop)
    count = local_energies * lax.axis_size("energy")
    peers = lax.axis_size("energy")
    outgoing = coupled.reshape(peers, 2, local_energies * comps // 2)
    mine = lax.dynamic_slice_in_dim(owner[:, 0], lax.axis_index("energy"), 1)
    mine, outgoing = lax.optimization_barrier((mine, outgoing))
    columns = lax.all_to_all(outgoing, "energy", split_axis=0, concat_axis=0, tiled=True)
    product = toeplitz_apply(mine, phonon, columns.reshape(count, comps))
    result = lax.all_to_all(
        product.reshape(count, ATOMS_DEV, comps), "energy", split_axis=0, concat_axis=1, tiled=True
    )
    return result


def solution(mesh):
    return jax.shard_map(
        per_device,
        mesh=mesh,
        in_specs=(P("energy", "atoms", None), P(), P(), P("atoms", None), P("atoms", None)),
        out_specs=P("energy", "atoms", None),
        check_vma=False,
    )
```

```python
import jax
import jax.numpy as jnp
from jax import lax
from jax.experimental import pallas as pl
from jax.experimental.pallas import tpu as pltpu
from jax.sharding import PartitionSpec as P

HALO = 8
EDGE = 8
ATOMS_DEV = 1


def toeplitz_kernel(owner_ref, phonon_ref, columns_ref, out_ref):
    count = columns_ref.shape[0]
    domain = owner_ref[0]
    base = pl.multiple_of((domain // 16) * 16, 16)
    block = phonon_ref[pl.ds(base, 16), :].astype(jnp.float32)
    rows = lax.broadcasted_iota(jnp.int32, block.shape, 0)
    row = jnp.sum(jnp.where(rows == domain - base, block, 0.0), axis=0, keepdims=True)
    wide = jnp.broadcast_to(row, (count, 2 * count))
    rolled = pltpu.roll(wide, shift=count, axis=1, stride=1, stride_axis=0)
    kernel_t = rolled[:, :count].astype(jnp.bfloat16)
    out_ref[...] = lax.dot_general(
        kernel_t, columns_ref[...], (((0,), (0,)), ((), ())), preferred_element_type=jnp.float32
    ).astype(out_ref.dtype)


def toeplitz_apply(owner, phonon, columns):
    count, comps = columns.shape
    vmem = pl.BlockSpec(memory_space=pltpu.VMEM)
    return pl.pallas_call(
        toeplitz_kernel,
        out_shape=jax.ShapeDtypeStruct((count, comps), jnp.bfloat16),
        in_specs=[pl.BlockSpec(memory_space=pltpu.SMEM), vmem, vmem],
        out_specs=vmem,
        cost_estimate=pl.CostEstimate(
            flops=2 * count * count * comps,
            bytes_accessed=2 * (phonon.size + 2 * count * comps),
            transcendentals=0,
        ),
    )(owner, phonon, columns)


def neighbour_kernel(neighbours_ref, low_ref, green_ref, high_ref, superop_ref, out_ref, rows_ref, picked_ref):
    width = low_ref.shape[0]
    atoms, energies, comps = green_ref.shape
    slots = superop_ref.shape[0]
    first = lax.axis_index("atoms") * atoms - width
    empty = 2 * width + atoms
    rows_ref[:width] = low_ref[...]
    rows_ref[width:width + atoms] = green_ref[...]
    rows_ref[width + atoms:2 * width + atoms] = high_ref[...]
    rows_ref[2 * width + atoms] = jnp.zeros((energies, comps), rows_ref.dtype)

    def pick(atom, carry):
        for slot in range(slots):
            target = neighbours_ref[atom, slot]
            row = jnp.where(target >= 0, target - first, empty)
            picked_ref[slot, atom] = rows_ref[row]
        return carry

    lax.fori_loop(0, atoms, pick, 0, unroll=8)
    total = jnp.zeros((atoms * energies, comps), jnp.float32)
    for slot in range(slots):
        total = total + jnp.dot(
            picked_ref[slot].reshape(atoms * energies, comps),
            superop_ref[slot],
            preferred_element_type=jnp.float32,
        )
    out_ref[...] = total.astype(out_ref.dtype).reshape(atoms, energies, comps)


def neighbour_apply(neighbours, low, green_t, high, superop):
    width = low.shape[0]
    atoms, energies, comps = green_t.shape
    slots = superop.shape[0]
    vmem = pl.BlockSpec(memory_space=pltpu.VMEM)
    return pl.pallas_call(
        neighbour_kernel,
        out_shape=jax.ShapeDtypeStruct(green_t.shape, jnp.bfloat16),
        in_specs=[pl.BlockSpec(memory_space=pltpu.SMEM)] + [vmem] * 4,
        out_specs=vmem,
        scratch_shapes=[
            pltpu.VMEM((2 * width + atoms + 1, energies, comps), jnp.bfloat16),
            pltpu.VMEM((slots, atoms, energies, comps), jnp.bfloat16),
        ],
        cost_estimate=pl.CostEstimate(
            flops=2 * slots * atoms * energies * comps * comps,
            bytes_accessed=2 * (2 * low.size + 2 * green_t.size + superop.size),
            transcendentals=0,
        ),
    )(neighbours, low, green_t, high, superop)


def per_device(green, superop, phonon, owner, neighbours):
    local_energies = green.shape[0]
    group_size = green.shape[1]
    comps = green.shape[2]
    groups = lax.axis_size("atoms")
    green_t = jnp.transpose(green, (1, 0, 2))
    forward = [(i, i + 1) for i in range(groups - 1)]
    backward = [(i + 1, i) for i in range(groups - 1)]
    low = lax.ppermute(green_t[group_size - EDGE:], "atoms", forward)
    high = lax.ppermute(green_t[:EDGE], "atoms", backward)
    coupled = neighbour_apply(neighbours, low, green_t, high, superop)
    count = local_energies * lax.axis_size("energy")
    peers = lax.axis_size("energy")
    outgoing = coupled.reshape(peers, 2, local_energies * comps // 2)
    mine = lax.dynamic_slice_in_dim(owner[:, 0], lax.axis_index("energy"), 1)
    mine, outgoing = lax.optimization_barrier((mine, outgoing))
    columns = lax.all_to_all(outgoing, "energy", split_axis=0, concat_axis=0, tiled=True)
    product = toeplitz_apply(mine, phonon, columns.reshape(count, comps))
    returning = product.reshape(peers, local_energies, comps).reshape(peers, 2, local_energies * comps // 2)
    result = lax.all_to_all(returning, "energy", split_axis=0, concat_axis=0, tiled=True)
    return jnp.transpose(result.reshape(peers, local_energies, comps), (1, 0, 2))


def solution(mesh):
    return jax.shard_map(
        per_device,
        mesh=mesh,
        in_specs=(P("energy", "atoms", None), P(), P(), P("atoms", None), P("atoms", None)),
        out_specs=P("energy", "atoms", None),
        check_vma=False,
    )
```

```python
import jax
import jax.numpy as jnp
from jax import lax
from jax.experimental import pallas as pl
from jax.experimental.pallas import tpu as pltpu
from jax.sharding import PartitionSpec as P

HALO = 8
EDGE = 8
ATOMS_DEV = 1


def store_packed(out_ref, blocks):
    energies, comps = blocks.shape[1], blocks.shape[2]
    half = energies // 2
    for h in range(2):
        for e in range(half):
            out_ref[:, h, e * comps:(e + 1) * comps] = blocks[:, h * half + e, :]


def load_packed(packed_ref, blocks_ref):
    energies, comps = blocks_ref.shape[1], blocks_ref.shape[2]
    half = energies // 2
    for h in range(2):
        for e in range(half):
            blocks_ref[:, h * half + e, :] = packed_ref[:, h, e * comps:(e + 1) * comps]


def unpack_kernel(packed_ref, out_ref):
    energies, comps = out_ref.shape[0], out_ref.shape[2]
    half = energies // 2
    for h in range(2):
        for e in range(half):
            out_ref[h * half + e] = packed_ref[:, h, e * comps:(e + 1) * comps]


def unpack(packed, energies):
    atoms = packed.shape[0]
    comps = packed.shape[2] * 2 // energies
    vmem = pl.BlockSpec(memory_space=pltpu.VMEM)
    return pl.pallas_call(
        unpack_kernel,
        out_shape=jax.ShapeDtypeStruct((energies, atoms, comps), packed.dtype),
        in_specs=[vmem],
        out_specs=vmem,
    )(packed)


def toeplitz_kernel(owner_ref, phonon_ref, packed_ref, out_ref, blocks_ref):
    peers, energies, comps = blocks_ref.shape
    count = peers * energies
    load_packed(packed_ref, blocks_ref)
    domain = owner_ref[0]
    base = pl.multiple_of((domain // 16) * 16, 16)
    block = phonon_ref[pl.ds(base, 16), :].astype(jnp.float32)
    rows = lax.broadcasted_iota(jnp.int32, block.shape, 0)
    row = jnp.sum(jnp.where(rows == domain - base, block, 0.0), axis=0, keepdims=True)
    wide = jnp.broadcast_to(row, (count, 2 * count))
    rolled = pltpu.roll(wide, shift=count, axis=1, stride=1, stride_axis=0)
    kernel_t = rolled[:, :count].astype(jnp.bfloat16)
    product = lax.dot_general(
        kernel_t, blocks_ref[...].reshape(count, comps), (((0,), (0,)), ((), ())),
        preferred_element_type=jnp.float32,
    )
    store_packed(out_ref, product.astype(out_ref.dtype).reshape(peers, energies, comps))


def toeplitz_apply(owner, phonon, packed, energies):
    peers = packed.shape[0]
    comps = packed.shape[2] * 2 // energies
    count = peers * energies
    vmem = pl.BlockSpec(memory_space=pltpu.VMEM)
    return pl.pallas_call(
        toeplitz_kernel,
        out_shape=jax.ShapeDtypeStruct(packed.shape, jnp.bfloat16),
        in_specs=[pl.BlockSpec(memory_space=pltpu.SMEM), vmem, vmem],
        out_specs=vmem,
        scratch_shapes=[pltpu.VMEM((peers, energies, comps), jnp.bfloat16)],
        cost_estimate=pl.CostEstimate(
            flops=2 * count * count * comps,
            bytes_accessed=2 * (phonon.size + 2 * count * comps),
            transcendentals=0,
        ),
    )(owner, phonon, packed)


def neighbour_kernel(neighbours_ref, low_ref, green_ref, high_ref, superop_ref, out_ref, rows_ref, picked_ref):
    width = low_ref.shape[0]
    atoms, energies, comps = green_ref.shape
    slots = superop_ref.shape[0]
    first = lax.axis_index("atoms") * atoms - width
    empty = 2 * width + atoms
    rows_ref[:width] = low_ref[...]
    rows_ref[width:width + atoms] = green_ref[...]
    rows_ref[width + atoms:2 * width + atoms] = high_ref[...]
    rows_ref[2 * width + atoms] = jnp.zeros((energies, comps), rows_ref.dtype)

    def pick(atom, carry):
        for slot in range(slots):
            target = neighbours_ref[atom, slot]
            row = jnp.where(target >= 0, target - first, empty)
            picked_ref[slot, atom] = rows_ref[row]
        return carry

    lax.fori_loop(0, atoms, pick, 0, unroll=8)
    total = jnp.zeros((atoms * energies, comps), jnp.float32)
    for slot in range(slots):
        total = total + jnp.dot(
            picked_ref[slot].reshape(atoms * energies, comps),
            superop_ref[slot],
            preferred_element_type=jnp.float32,
        )
    store_packed(out_ref, total.astype(out_ref.dtype).reshape(atoms, energies, comps))


def neighbour_apply(neighbours, low, green_t, high, superop):
    width = low.shape[0]
    atoms, energies, comps = green_t.shape
    slots = superop.shape[0]
    vmem = pl.BlockSpec(memory_space=pltpu.VMEM)
    return pl.pallas_call(
        neighbour_kernel,
        out_shape=jax.ShapeDtypeStruct((atoms, 2, energies * comps // 2), jnp.bfloat16),
        in_specs=[pl.BlockSpec(memory_space=pltpu.SMEM)] + [vmem] * 4,
        out_specs=vmem,
        scratch_shapes=[
            pltpu.VMEM((2 * width + atoms + 1, energies, comps), jnp.bfloat16),
            pltpu.VMEM((slots, atoms, energies, comps), jnp.bfloat16),
        ],
        cost_estimate=pl.CostEstimate(
            flops=2 * slots * atoms * energies * comps * comps,
            bytes_accessed=2 * (2 * low.size + 2 * green_t.size + superop.size),
            transcendentals=0,
        ),
    )(neighbours, low, green_t, high, superop)


def per_device(green, superop, phonon, owner, neighbours):
    local_energies = green.shape[0]
    group_size = green.shape[1]
    comps = green.shape[2]
    groups = lax.axis_size("atoms")
    green_t = jnp.transpose(green, (1, 0, 2))
    forward = [(i, i + 1) for i in range(groups - 1)]
    backward = [(i + 1, i) for i in range(groups - 1)]
    low = lax.ppermute(green_t[group_size - EDGE:], "atoms", forward)
    high = lax.ppermute(green_t[:EDGE], "atoms", backward)
    outgoing = neighbour_apply(neighbours, low, green_t, high, superop)
    mine = lax.dynamic_slice_in_dim(owner[:, 0], lax.axis_index("energy"), 1)
    mine, outgoing = lax.optimization_barrier((mine, outgoing))
    columns = lax.all_to_all(outgoing, "energy", split_axis=0, concat_axis=0, tiled=True)
    product = toeplitz_apply(mine, phonon, columns, local_energies)
    result = lax.all_to_all(product, "energy", split_axis=0, concat_axis=0, tiled=True)
    return unpack(result, local_energies)


def solution(mesh):
    return jax.shard_map(
        per_device,
        mesh=mesh,
        in_specs=(P("energy", "atoms", None), P(), P(), P("atoms", None), P("atoms", None)),
        out_specs=P("energy", "atoms", None),
        check_vma=False,
    )
```

```python
import jax
import jax.numpy as jnp
from jax import lax
from jax.experimental import pallas as pl
from jax.experimental.pallas import tpu as pltpu
from jax.sharding import PartitionSpec as P

HALO = 8
EDGE = 8
ATOMS_DEV = 1


def store_packed(out_ref, blocks):
    energies, comps = blocks.shape[1], blocks.shape[2]
    half = energies // 2
    for h in range(2):
        for e in range(half):
            out_ref[:, h, e * comps:(e + 1) * comps] = blocks[:, h * half + e, :]


def load_packed(packed_ref, blocks_ref):
    energies, comps = blocks_ref.shape[1], blocks_ref.shape[2]
    half = energies // 2
    for h in range(2):
        for e in range(half):
            blocks_ref[:, h * half + e, :] = packed_ref[:, h, e * comps:(e + 1) * comps]


def toeplitz_kernel(owner_ref, phonon_ref, packed_ref, out_ref, blocks_ref):
    peers, energies, comps = blocks_ref.shape
    count = peers * energies
    load_packed(packed_ref, blocks_ref)
    domain = owner_ref[0]
    base = pl.multiple_of((domain // 16) * 16, 16)
    block = phonon_ref[pl.ds(base, 16), :].astype(jnp.float32)
    rows = lax.broadcasted_iota(jnp.int32, block.shape, 0)
    row = jnp.sum(jnp.where(rows == domain - base, block, 0.0), axis=0, keepdims=True)
    wide = jnp.broadcast_to(row, (count, 2 * count))
    rolled = pltpu.roll(wide, shift=count, axis=1, stride=1, stride_axis=0)
    kernel_t = rolled[:, :count].astype(jnp.bfloat16)
    product = lax.dot_general(
        kernel_t, blocks_ref[...].reshape(count, comps), (((0,), (0,)), ((), ())),
        preferred_element_type=jnp.float32,
    )
    store_packed(out_ref, product.astype(out_ref.dtype).reshape(peers, energies, comps))


def toeplitz_apply(owner, phonon, packed, energies):
    peers = packed.shape[0]
    comps = packed.shape[2] * 2 // energies
    count = peers * energies
    vmem = pl.BlockSpec(memory_space=pltpu.VMEM)
    return pl.pallas_call(
        toeplitz_kernel,
        out_shape=jax.ShapeDtypeStruct(packed.shape, jnp.bfloat16),
        in_specs=[pl.BlockSpec(memory_space=pltpu.SMEM), vmem, vmem],
        out_specs=vmem,
        scratch_shapes=[pltpu.VMEM((peers, energies, comps), jnp.bfloat16)],
        cost_estimate=pl.CostEstimate(
            flops=2 * count * count * comps,
            bytes_accessed=2 * (phonon.size + 2 * count * comps),
            transcendentals=0,
        ),
    )(owner, phonon, packed)


def neighbour_kernel(neighbours_ref, low_ref, green_ref, high_ref, superop_ref, out_ref, rows_ref, picked_ref):
    width = low_ref.shape[0]
    atoms, energies, comps = green_ref.shape
    slots = superop_ref.shape[0]
    first = lax.axis_index("atoms") * atoms - width
    empty = 2 * width + atoms
    rows_ref[:width] = low_ref[...]
    rows_ref[width:width + atoms] = green_ref[...]
    rows_ref[width + atoms:2 * width + atoms] = high_ref[...]
    rows_ref[2 * width + atoms] = jnp.zeros((energies, comps), rows_ref.dtype)

    def pick(atom, carry):
        for slot in range(slots):
            target = neighbours_ref[atom, slot]
            row = jnp.where(target >= 0, target - first, empty)
            picked_ref[slot, atom] = rows_ref[row]
        return carry

    lax.fori_loop(0, atoms, pick, 0, unroll=8)
    total = jnp.zeros((atoms * energies, comps), jnp.float32)
    for slot in range(slots):
        total = total + jnp.dot(
            picked_ref[slot].reshape(atoms * energies, comps),
            superop_ref[slot],
            preferred_element_type=jnp.float32,
        )
    store_packed(out_ref, total.astype(out_ref.dtype).reshape(atoms, energies, comps))


def neighbour_apply(neighbours, low, green_t, high, superop):
    width = low.shape[0]
    atoms, energies, comps = green_t.shape
    slots = superop.shape[0]
    vmem = pl.BlockSpec(memory_space=pltpu.VMEM)
    return pl.pallas_call(
        neighbour_kernel,
        out_shape=jax.ShapeDtypeStruct((atoms, 2, energies * comps // 2), jnp.bfloat16),
        in_specs=[pl.BlockSpec(memory_space=pltpu.SMEM)] + [vmem] * 4,
        out_specs=vmem,
        scratch_shapes=[
            pltpu.VMEM((2 * width + atoms + 1, energies, comps), jnp.bfloat16),
            pltpu.VMEM((slots, atoms, energies, comps), jnp.bfloat16),
        ],
        cost_estimate=pl.CostEstimate(
            flops=2 * slots * atoms * energies * comps * comps,
            bytes_accessed=2 * (2 * low.size + 2 * green_t.size + superop.size),
            transcendentals=0,
        ),
    )(neighbours, low, green_t, high, superop)


def per_device(green, superop, phonon, owner, neighbours):
    local_energies = green.shape[0]
    group_size = green.shape[1]
    comps = green.shape[2]
    groups = lax.axis_size("atoms")
    green_t = jnp.transpose(green, (1, 0, 2))
    forward = [(i, i + 1) for i in range(groups - 1)]
    backward = [(i + 1, i) for i in range(groups - 1)]
    low = lax.ppermute(green_t[group_size - EDGE:], "atoms", forward)
    high = lax.ppermute(green_t[:EDGE], "atoms", backward)
    outgoing = neighbour_apply(neighbours, low, green_t, high, superop)
    mine = lax.dynamic_slice_in_dim(owner[:, 0], lax.axis_index("energy"), 1)
    mine, outgoing = lax.optimization_barrier((mine, outgoing))
    columns = lax.all_to_all(outgoing, "energy", split_axis=0, concat_axis=0, tiled=True)
    product = toeplitz_apply(mine, phonon, columns, local_energies)
    result = lax.all_to_all(product, "energy", split_axis=0, concat_axis=0, tiled=True)
    result = result.reshape(result.shape[0], local_energies, comps)
    return jnp.transpose(result, (1, 0, 2))


def solution(mesh):
    return jax.shard_map(
        per_device,
        mesh=mesh,
        in_specs=(P("energy", "atoms", None), P(), P(), P("atoms", None), P("atoms", None)),
        out_specs=P("energy", "atoms", None),
        check_vma=False,
    )
```

```python
import jax
import jax.numpy as jnp
from jax import lax
from jax.experimental import pallas as pl
from jax.experimental.pallas import tpu as pltpu
from jax.sharding import PartitionSpec as P

HALO = 8
EDGE = 8
ATOMS_DEV = 1


def store_packed(out_ref, blocks):
    energies, comps = blocks.shape[1], blocks.shape[2]
    half = energies // 2
    for h in range(2):
        for e in range(half):
            out_ref[:, h, e * comps:(e + 1) * comps] = blocks[:, h * half + e, :]


def load_packed(packed_ref, blocks_ref):
    energies, comps = blocks_ref.shape[1], blocks_ref.shape[2]
    half = energies // 2
    for h in range(2):
        for e in range(half):
            blocks_ref[:, h * half + e, :] = packed_ref[:, h, e * comps:(e + 1) * comps]


def toeplitz_kernel(owner_ref, phonon_ref, packed_ref, out_ref, blocks_ref):
    peers, energies, comps = blocks_ref.shape
    count = peers * energies
    load_packed(packed_ref, blocks_ref)
    domain = owner_ref[0, lax.axis_index("energy")]
    base = pl.multiple_of((domain // 16) * 16, 16)
    block = phonon_ref[pl.ds(base, 16), :].astype(jnp.float32)
    rows = lax.broadcasted_iota(jnp.int32, block.shape, 0)
    row = jnp.sum(jnp.where(rows == domain - base, block, 0.0), axis=0, keepdims=True)
    wide = jnp.broadcast_to(row, (count, 2 * count))
    rolled = pltpu.roll(wide, shift=count, axis=1, stride=1, stride_axis=0)
    kernel_t = rolled[:, :count].astype(jnp.bfloat16)
    product = lax.dot_general(
        kernel_t, blocks_ref[...].reshape(count, comps), (((0,), (0,)), ((), ())),
        preferred_element_type=jnp.float32,
    )
    store_packed(out_ref, product.astype(out_ref.dtype).reshape(peers, energies, comps))


def toeplitz_apply(owner, phonon, packed, energies):
    peers = packed.shape[0]
    comps = packed.shape[2] * 2 // energies
    count = peers * energies
    vmem = pl.BlockSpec(memory_space=pltpu.VMEM)
    return pl.pallas_call(
        toeplitz_kernel,
        out_shape=jax.ShapeDtypeStruct(packed.shape, jnp.bfloat16),
        in_specs=[pl.BlockSpec(memory_space=pltpu.SMEM), vmem, vmem],
        out_specs=vmem,
        scratch_shapes=[pltpu.VMEM((peers, energies, comps), jnp.bfloat16)],
        cost_estimate=pl.CostEstimate(
            flops=2 * count * count * comps,
            bytes_accessed=2 * (phonon.size + 2 * count * comps),
            transcendentals=0,
        ),
    )(owner, phonon, packed)


def neighbour_kernel(neighbours_ref, low_ref, green_ref, high_ref, superop_ref, out_ref, rows_ref, picked_ref):
    width = low_ref.shape[1]
    atoms, energies, comps = green_ref.shape
    slots = superop_ref.shape[0]
    first = lax.axis_index("atoms") * atoms - width
    empty = 2 * width + atoms
    rows_ref[width:width + atoms] = green_ref[...]
    for atom in range(width):
        rows_ref[atom] = low_ref[:, atom, :]
        rows_ref[width + atoms + atom] = high_ref[:, atom, :]
    rows_ref[2 * width + atoms] = jnp.zeros((energies, comps), rows_ref.dtype)

    def pick(atom, carry):
        for slot in range(slots):
            target = neighbours_ref[slot, atom]
            row = jnp.where(target >= 0, target - first, empty)
            picked_ref[slot, atom] = rows_ref[row]
        return carry

    lax.fori_loop(0, atoms, pick, 0, unroll=8)
    total = jnp.zeros((atoms * energies, comps), jnp.float32)
    for slot in range(slots):
        total = total + jnp.dot(
            picked_ref[slot].reshape(atoms * energies, comps),
            superop_ref[slot],
            preferred_element_type=jnp.float32,
        )
    store_packed(out_ref, total.astype(out_ref.dtype).reshape(atoms, energies, comps))


def neighbour_apply(neighbours, low, green_t, high, superop):
    width = low.shape[1]
    atoms, energies, comps = green_t.shape
    slots = superop.shape[0]
    vmem = pl.BlockSpec(memory_space=pltpu.VMEM)
    return pl.pallas_call(
        neighbour_kernel,
        out_shape=jax.ShapeDtypeStruct((atoms, 2, energies * comps // 2), jnp.bfloat16),
        in_specs=[pl.BlockSpec(memory_space=pltpu.SMEM)] + [vmem] * 4,
        out_specs=vmem,
        scratch_shapes=[
            pltpu.VMEM((2 * width + atoms + 1, energies, comps), jnp.bfloat16),
            pltpu.VMEM((slots, atoms, energies, comps), jnp.bfloat16),
        ],
        cost_estimate=pl.CostEstimate(
            flops=2 * slots * atoms * energies * comps * comps,
            bytes_accessed=2 * (2 * low.size + 2 * green_t.size + superop.size),
            transcendentals=0,
        ),
    )(neighbours, low, green_t, high, superop)


def per_device(green, superop, phonon, owner, neighbours):
    local_energies = green.shape[0]
    group_size = green.shape[1]
    comps = green.shape[2]
    groups = lax.axis_size("atoms")
    green_t = jnp.transpose(green, (1, 0, 2))
    forward = [(i, i + 1) for i in range(groups - 1)]
    backward = [(i + 1, i) for i in range(groups - 1)]
    low = lax.ppermute(green[:, group_size - EDGE:], "atoms", forward)
    high = lax.ppermute(green[:, :EDGE], "atoms", backward)
    outgoing = neighbour_apply(neighbours.T, low, green_t, high, superop)
    owner_t, outgoing = lax.optimization_barrier((owner.T, outgoing))
    columns = lax.all_to_all(outgoing, "energy", split_axis=0, concat_axis=0, tiled=True)
    product = toeplitz_apply(owner_t, phonon, columns, local_energies)
    result = lax.all_to_all(product, "energy", split_axis=0, concat_axis=0, tiled=True)
    result = result.reshape(result.shape[0], local_energies, comps)
    return jnp.transpose(result, (1, 0, 2))


def solution(mesh):
    return jax.shard_map(
        per_device,
        mesh=mesh,
        in_specs=(P("energy", "atoms", None), P(), P(), P("atoms", None), P("atoms", None)),
        out_specs=P("energy", "atoms", None),
        check_vma=False,
    )
```

```python
import jax
import jax.numpy as jnp
from jax import lax
from jax.experimental import pallas as pl
from jax.experimental.pallas import tpu as pltpu
from jax.sharding import PartitionSpec as P

HALO = 8
EDGE = 8
ATOMS_DEV = 1


def store_packed(out_ref, blocks):
    energies, comps = blocks.shape[1], blocks.shape[2]
    half = energies // 2
    for h in range(2):
        for e in range(half):
            out_ref[:, h, e * comps:(e + 1) * comps] = blocks[:, h * half + e, :]


def load_packed(packed_ref, blocks_ref):
    energies, comps = blocks_ref.shape[1], blocks_ref.shape[2]
    half = energies // 2
    for h in range(2):
        for e in range(half):
            blocks_ref[:, h * half + e, :] = packed_ref[:, h, e * comps:(e + 1) * comps]


def toeplitz_kernel(owner_ref, phonon_ref, packed_ref, out_ref, blocks_ref):
    peers, energies, comps = blocks_ref.shape
    count = peers * energies
    load_packed(packed_ref, blocks_ref)
    domain = owner_ref[0, lax.axis_index("energy")]
    base = pl.multiple_of((domain // 16) * 16, 16)
    block = phonon_ref[pl.ds(base, 16), :].astype(jnp.float32)
    rows = lax.broadcasted_iota(jnp.int32, block.shape, 0)
    row = jnp.sum(jnp.where(rows == domain - base, block, 0.0), axis=0, keepdims=True)
    wide = jnp.broadcast_to(row, (count, 2 * count))
    rolled = pltpu.roll(wide, shift=count, axis=1, stride=1, stride_axis=0)
    kernel_t = rolled[:, :count].astype(jnp.bfloat16)
    product = lax.dot_general(
        kernel_t, blocks_ref[...].reshape(count, comps), (((0,), (0,)), ((), ())),
        preferred_element_type=jnp.float32,
    )
    store_packed(out_ref, product.astype(out_ref.dtype).reshape(peers, energies, comps))


def toeplitz_apply(owner, phonon, packed, energies):
    peers = packed.shape[0]
    comps = packed.shape[2] * 2 // energies
    count = peers * energies
    vmem = pl.BlockSpec(memory_space=pltpu.VMEM)
    return pl.pallas_call(
        toeplitz_kernel,
        out_shape=jax.ShapeDtypeStruct(packed.shape, jnp.bfloat16),
        in_specs=[pl.BlockSpec(memory_space=pltpu.SMEM), vmem, vmem],
        out_specs=vmem,
        scratch_shapes=[pltpu.VMEM((peers, energies, comps), jnp.bfloat16)],
        cost_estimate=pl.CostEstimate(
            flops=2 * count * count * comps,
            bytes_accessed=2 * (phonon.size + 2 * count * comps),
            transcendentals=0,
        ),
    )(owner, phonon, packed)


def neighbour_kernel(neighbours_ref, low_ref, green_ref, high_ref, superop_ref, out_ref, rows_ref, picked_ref):
    width = low_ref.shape[1]
    energies, atoms, comps = green_ref.shape
    slots = superop_ref.shape[0]
    first = lax.axis_index("atoms") * atoms - width
    empty = 2 * width + atoms
    for atom in range(atoms):
        rows_ref[width + atom] = green_ref[:, atom, :]
    for atom in range(width):
        rows_ref[atom] = low_ref[:, atom, :]
        rows_ref[width + atoms + atom] = high_ref[:, atom, :]
    rows_ref[2 * width + atoms] = jnp.zeros((energies, comps), rows_ref.dtype)

    def pick(atom, carry):
        for slot in range(slots):
            target = neighbours_ref[slot, atom]
            row = jnp.where(target >= 0, target - first, empty)
            picked_ref[slot, atom] = rows_ref[row]
        return carry

    lax.fori_loop(0, atoms, pick, 0, unroll=8)
    total = jnp.zeros((atoms * energies, comps), jnp.float32)
    for slot in range(slots):
        total = total + jnp.dot(
            picked_ref[slot].reshape(atoms * energies, comps),
            superop_ref[slot],
            preferred_element_type=jnp.float32,
        )
    store_packed(out_ref, total.astype(out_ref.dtype).reshape(atoms, energies, comps))


def neighbour_apply(neighbours, low, green, high, superop):
    width = low.shape[1]
    energies, atoms, comps = green.shape
    slots = superop.shape[0]
    vmem = pl.BlockSpec(memory_space=pltpu.VMEM)
    return pl.pallas_call(
        neighbour_kernel,
        out_shape=jax.ShapeDtypeStruct((atoms, 2, energies * comps // 2), jnp.bfloat16),
        in_specs=[pl.BlockSpec(memory_space=pltpu.SMEM)] + [vmem] * 4,
        out_specs=vmem,
        scratch_shapes=[
            pltpu.VMEM((2 * width + atoms + 1, energies, comps), jnp.bfloat16),
            pltpu.VMEM((slots, atoms, energies, comps), jnp.bfloat16),
        ],
        cost_estimate=pl.CostEstimate(
            flops=2 * slots * atoms * energies * comps * comps,
            bytes_accessed=2 * (2 * low.size + 2 * green.size + superop.size),
            transcendentals=0,
        ),
    )(neighbours, low, green, high, superop)


def per_device(green, superop, phonon, owner, neighbours):
    local_energies = green.shape[0]
    group_size = green.shape[1]
    comps = green.shape[2]
    groups = lax.axis_size("atoms")
    forward = [(i, i + 1) for i in range(groups - 1)]
    backward = [(i + 1, i) for i in range(groups - 1)]
    low = lax.ppermute(green[:, group_size - EDGE:], "atoms", forward)
    high = lax.ppermute(green[:, :EDGE], "atoms", backward)
    outgoing = neighbour_apply(neighbours.T, low, green, high, superop)
    owner_t, outgoing = lax.optimization_barrier((owner.T, outgoing))
    columns = lax.all_to_all(outgoing, "energy", split_axis=0, concat_axis=0, tiled=True)
    product = toeplitz_apply(owner_t, phonon, columns, local_energies)
    result = lax.all_to_all(product, "energy", split_axis=0, concat_axis=0, tiled=True)
    result = result.reshape(result.shape[0], local_energies, comps)
    return jnp.transpose(result, (1, 0, 2))


def solution(mesh):
    return jax.shard_map(
        per_device,
        mesh=mesh,
        in_specs=(P("energy", "atoms", None), P(), P(), P("atoms", None), P("atoms", None)),
        out_specs=P("energy", "atoms", None),
        check_vma=False,
    )
```

```python
import jax
import jax.numpy as jnp
from jax import lax
from jax.experimental import pallas as pl
from jax.experimental.pallas import tpu as pltpu
from jax.sharding import PartitionSpec as P

HALO = 8
EDGE = 8
ATOMS_DEV = 1


def store_packed(out_ref, blocks):
    energies, comps = blocks.shape[1], blocks.shape[2]
    half = energies // 2
    for h in range(2):
        for e in range(half):
            out_ref[:, h, e * comps:(e + 1) * comps] = blocks[:, h * half + e, :]


def load_packed(packed_ref, blocks_ref):
    energies, comps = blocks_ref.shape[1], blocks_ref.shape[2]
    half = energies // 2
    for h in range(2):
        for e in range(half):
            blocks_ref[:, h * half + e, :] = packed_ref[:, h, e * comps:(e + 1) * comps]


def toeplitz_kernel(owner_ref, phonon_ref, packed_ref, out_ref, blocks_ref):
    peers, energies, comps = blocks_ref.shape
    count = peers * energies
    load_packed(packed_ref, blocks_ref)
    domain = owner_ref[0, lax.axis_index("energy")]
    base = pl.multiple_of((domain // 16) * 16, 16)
    block = phonon_ref[pl.ds(base, 16), :].astype(jnp.float32)
    rows = lax.broadcasted_iota(jnp.int32, block.shape, 0)
    row = jnp.sum(jnp.where(rows == domain - base, block, 0.0), axis=0, keepdims=True)
    wide = jnp.broadcast_to(row.astype(jnp.bfloat16), (count, 2 * count))
    rolled = pltpu.roll(wide, shift=count, axis=1, stride=1, stride_axis=0)
    kernel_t = rolled[:, :count]
    product = lax.dot_general(
        kernel_t, blocks_ref[...].reshape(count, comps), (((0,), (0,)), ((), ())),
        preferred_element_type=jnp.float32,
    )
    store_packed(out_ref, product.astype(out_ref.dtype).reshape(peers, energies, comps))


def toeplitz_apply(owner, phonon, packed, energies):
    peers = packed.shape[0]
    comps = packed.shape[2] * 2 // energies
    count = peers * energies
    vmem = pl.BlockSpec(memory_space=pltpu.VMEM)
    return pl.pallas_call(
        toeplitz_kernel,
        out_shape=jax.ShapeDtypeStruct(packed.shape, jnp.bfloat16),
        in_specs=[pl.BlockSpec(memory_space=pltpu.SMEM), vmem, vmem],
        out_specs=vmem,
        scratch_shapes=[pltpu.VMEM((peers, energies, comps), jnp.bfloat16)],
        cost_estimate=pl.CostEstimate(
            flops=2 * count * count * comps,
            bytes_accessed=2 * (phonon.size + 2 * count * comps),
            transcendentals=0,
        ),
    )(owner, phonon, packed)


def neighbour_kernel(neighbours_ref, low_ref, green_ref, high_ref, superop_ref, out_ref, rows_ref, picked_ref):
    width = low_ref.shape[1]
    atoms, energies, comps = green_ref.shape
    slots = superop_ref.shape[0]
    first = lax.axis_index("atoms") * atoms - width
    empty = 2 * width + atoms
    rows_ref[width:width + atoms] = green_ref[...]
    for atom in range(width):
        rows_ref[atom] = low_ref[:, atom, :]
        rows_ref[width + atoms + atom] = high_ref[:, atom, :]
    rows_ref[2 * width + atoms] = jnp.zeros((energies, comps), rows_ref.dtype)

    def pick(atom, carry):
        for slot in range(slots):
            target = neighbours_ref[slot, atom]
            row = jnp.where(target >= 0, target - first, empty)
            picked_ref[slot, atom] = rows_ref[row]
        return carry

    lax.fori_loop(0, atoms, pick, 0, unroll=True)
    total = jnp.zeros((atoms * energies, comps), jnp.float32)
    for slot in range(slots):
        total = total + jnp.dot(
            picked_ref[slot].reshape(atoms * energies, comps),
            superop_ref[slot],
            preferred_element_type=jnp.float32,
        )
    store_packed(out_ref, total.astype(out_ref.dtype).reshape(atoms, energies, comps))


def neighbour_apply(neighbours, low, green_t, high, superop):
    width = low.shape[1]
    atoms, energies, comps = green_t.shape
    slots = superop.shape[0]
    vmem = pl.BlockSpec(memory_space=pltpu.VMEM)
    return pl.pallas_call(
        neighbour_kernel,
        out_shape=jax.ShapeDtypeStruct((atoms, 2, energies * comps // 2), jnp.bfloat16),
        in_specs=[pl.BlockSpec(memory_space=pltpu.SMEM)] + [vmem] * 4,
        out_specs=vmem,
        scratch_shapes=[
            pltpu.VMEM((2 * width + atoms + 1, energies, comps), jnp.bfloat16),
            pltpu.VMEM((slots, atoms, energies, comps), jnp.bfloat16),
        ],
        cost_estimate=pl.CostEstimate(
            flops=2 * slots * atoms * energies * comps * comps,
            bytes_accessed=2 * (2 * low.size + 2 * green_t.size + superop.size),
            transcendentals=0,
        ),
    )(neighbours, low, green_t, high, superop)


def per_device(green, superop, phonon, owner, neighbours):
    local_energies = green.shape[0]
    group_size = green.shape[1]
    comps = green.shape[2]
    groups = lax.axis_size("atoms")
    green_t = jnp.transpose(green, (1, 0, 2))
    forward = [(i, i + 1) for i in range(groups - 1)]
    backward = [(i + 1, i) for i in range(groups - 1)]
    low = lax.ppermute(green[:, group_size - EDGE:], "atoms", forward)
    high = lax.ppermute(green[:, :EDGE], "atoms", backward)
    outgoing = neighbour_apply(neighbours.T, low, green_t, high, superop)
    owner_t, outgoing = lax.optimization_barrier((owner.T, outgoing))
    columns = lax.all_to_all(outgoing, "energy", split_axis=0, concat_axis=0, tiled=True)
    product = toeplitz_apply(owner_t, phonon, columns, local_energies)
    result = lax.all_to_all(product, "energy", split_axis=0, concat_axis=0, tiled=True)
    result = result.reshape(result.shape[0], local_energies, comps)
    return jnp.transpose(result, (1, 0, 2))


def solution(mesh):
    return jax.shard_map(
        per_device,
        mesh=mesh,
        in_specs=(P("energy", "atoms", None), P(), P(), P("atoms", None), P("atoms", None)),
        out_specs=P("energy", "atoms", None),
        check_vma=False,
    )
```

```python
import jax
import jax.numpy as jnp
from jax import lax
from jax.experimental import pallas as pl
from jax.experimental.pallas import tpu as pltpu
from jax.sharding import PartitionSpec as P

HALO = 8
EDGE = 8
ATOMS_DEV = 1


def store_packed(out_ref, blocks):
    energies, comps = blocks.shape[1], blocks.shape[2]
    half = energies // 2
    for h in range(2):
        for e in range(half):
            out_ref[:, h, e * comps:(e + 1) * comps] = blocks[:, h * half + e, :]


def load_packed(packed_ref, blocks_ref):
    energies, comps = blocks_ref.shape[1], blocks_ref.shape[2]
    half = energies // 2
    for h in range(2):
        for e in range(half):
            blocks_ref[:, h * half + e, :] = packed_ref[:, h, e * comps:(e + 1) * comps]


def toeplitz_build_kernel(owner_ref, phonon_ref, out_ref):
    count = out_ref.shape[0]
    domain = owner_ref[0, lax.axis_index("energy")]
    base = pl.multiple_of((domain // 16) * 16, 16)
    block = phonon_ref[pl.ds(base, 16), :].astype(jnp.float32)
    rows = lax.broadcasted_iota(jnp.int32, block.shape, 0)
    row = jnp.sum(jnp.where(rows == domain - base, block, 0.0), axis=0, keepdims=True)
    wide = jnp.broadcast_to(row.astype(jnp.bfloat16), (count, 2 * count))
    rolled = pltpu.roll(wide, shift=count, axis=1, stride=1, stride_axis=0)
    out_ref[...] = rolled[:, :count]


def toeplitz_build(owner, phonon, count):
    return pl.pallas_call(
        toeplitz_build_kernel,
        out_shape=jax.ShapeDtypeStruct((count, count), jnp.bfloat16),
        in_specs=[pl.BlockSpec(memory_space=pltpu.SMEM), pl.BlockSpec(memory_space=pltpu.VMEM)],
        out_specs=pl.BlockSpec(memory_space=pltpu.VMEM),
        cost_estimate=pl.CostEstimate(
            flops=0, bytes_accessed=2 * (phonon.size + count * count), transcendentals=0
        ),
    )(owner, phonon)


def toeplitz_kernel(kernel_ref, packed_ref, out_ref, blocks_ref):
    peers, energies, comps = blocks_ref.shape
    count = peers * energies
    load_packed(packed_ref, blocks_ref)
    product = lax.dot_general(
        kernel_ref[...], blocks_ref[...].reshape(count, comps), (((0,), (0,)), ((), ())),
        preferred_element_type=jnp.float32,
    )
    store_packed(out_ref, product.astype(out_ref.dtype).reshape(peers, energies, comps))


def toeplitz_apply(kernel_t, packed, energies):
    peers = packed.shape[0]
    comps = packed.shape[2] * 2 // energies
    count = peers * energies
    vmem = pl.BlockSpec(memory_space=pltpu.VMEM)
    return pl.pallas_call(
        toeplitz_kernel,
        out_shape=jax.ShapeDtypeStruct(packed.shape, jnp.bfloat16),
        in_specs=[vmem, vmem],
        out_specs=vmem,
        scratch_shapes=[pltpu.VMEM((peers, energies, comps), jnp.bfloat16)],
        cost_estimate=pl.CostEstimate(
            flops=2 * count * count * comps,
            bytes_accessed=2 * (count * count + 2 * count * comps),
            transcendentals=0,
        ),
    )(kernel_t, packed)


def neighbour_kernel(neighbours_ref, low_ref, green_ref, high_ref, superop_ref, out_ref, rows_ref, picked_ref):
    width = low_ref.shape[1]
    atoms, energies, comps = green_ref.shape
    slots = superop_ref.shape[0]
    first = lax.axis_index("atoms") * atoms - width
    empty = 2 * width + atoms
    rows_ref[width:width + atoms] = green_ref[...]
    for atom in range(width):
        rows_ref[atom] = low_ref[:, atom, :]
        rows_ref[width + atoms + atom] = high_ref[:, atom, :]
    rows_ref[2 * width + atoms] = jnp.zeros((energies, comps), rows_ref.dtype)

    def pick(atom, carry):
        for slot in range(slots):
            target = neighbours_ref[slot, atom]
            row = jnp.where(target >= 0, target - first, empty)
            picked_ref[slot, atom] = rows_ref[row]
        return carry

    lax.fori_loop(0, atoms, pick, 0, unroll=True)
    total = jnp.zeros((atoms * energies, comps), jnp.float32)
    for slot in range(slots):
        total = total + jnp.dot(
            picked_ref[slot].reshape(atoms * energies, comps),
            superop_ref[slot],
            preferred_element_type=jnp.float32,
        )
    store_packed(out_ref, total.astype(out_ref.dtype).reshape(atoms, energies, comps))


def neighbour_apply(neighbours, low, green_t, high, superop):
    width = low.shape[1]
    atoms, energies, comps = green_t.shape
    slots = superop.shape[0]
    vmem = pl.BlockSpec(memory_space=pltpu.VMEM)
    return pl.pallas_call(
        neighbour_kernel,
        out_shape=jax.ShapeDtypeStruct((atoms, 2, energies * comps // 2), jnp.bfloat16),
        in_specs=[pl.BlockSpec(memory_space=pltpu.SMEM)] + [vmem] * 4,
        out_specs=vmem,
        scratch_shapes=[
            pltpu.VMEM((2 * width + atoms + 1, energies, comps), jnp.bfloat16),
            pltpu.VMEM((slots, atoms, energies, comps), jnp.bfloat16),
        ],
        cost_estimate=pl.CostEstimate(
            flops=2 * slots * atoms * energies * comps * comps,
            bytes_accessed=2 * (2 * low.size + 2 * green_t.size + superop.size),
            transcendentals=0,
        ),
    )(neighbours, low, green_t, high, superop)


def per_device(green, superop, phonon, owner, neighbours):
    local_energies = green.shape[0]
    group_size = green.shape[1]
    comps = green.shape[2]
    groups = lax.axis_size("atoms")
    green_t = jnp.transpose(green, (1, 0, 2))
    forward = [(i, i + 1) for i in range(groups - 1)]
    backward = [(i + 1, i) for i in range(groups - 1)]
    low = lax.ppermute(green[:, group_size - EDGE:], "atoms", forward)
    high = lax.ppermute(green[:, :EDGE], "atoms", backward)
    outgoing = neighbour_apply(neighbours.T, low, green_t, high, superop)
    count = local_energies * lax.axis_size("energy")
    kernel_t = toeplitz_build(owner.T, phonon, count)
    columns = lax.all_to_all(outgoing, "energy", split_axis=0, concat_axis=0, tiled=True)
    product = toeplitz_apply(kernel_t, columns, local_energies)
    result = lax.all_to_all(product, "energy", split_axis=0, concat_axis=0, tiled=True)
    result = result.reshape(result.shape[0], local_energies, comps)
    return jnp.transpose(result, (1, 0, 2))


def solution(mesh):
    return jax.shard_map(
        per_device,
        mesh=mesh,
        in_specs=(P("energy", "atoms", None), P(), P(), P("atoms", None), P("atoms", None)),
        out_specs=P("energy", "atoms", None),
        check_vma=False,
    )
```

```python
import jax
import jax.numpy as jnp
from jax import lax
from jax.experimental import pallas as pl
from jax.experimental.pallas import tpu as pltpu
from jax.sharding import PartitionSpec as P

HALO = 8
EDGE = 8
ATOMS_DEV = 1


def store_packed(out_ref, blocks):
    energies, comps = blocks.shape[1], blocks.shape[2]
    half = energies // 2
    for h in range(2):
        for e in range(half):
            out_ref[:, h, e * comps:(e + 1) * comps] = blocks[:, h * half + e, :]


def load_packed(packed_ref, blocks_ref):
    energies, comps = blocks_ref.shape[1], blocks_ref.shape[2]
    half = energies // 2
    for h in range(2):
        for e in range(half):
            blocks_ref[:, h * half + e, :] = packed_ref[:, h, e * comps:(e + 1) * comps]


def toeplitz_build_kernel(owner_ref, phonon_ref, out_ref):
    count = out_ref.shape[0]
    domain = owner_ref[0, lax.axis_index("energy")]
    base = pl.multiple_of((domain // 16) * 16, 16)
    block = phonon_ref[pl.ds(base, 16), :].astype(jnp.float32)
    rows = lax.broadcasted_iota(jnp.int32, block.shape, 0)
    row = jnp.sum(jnp.where(rows == domain - base, block, 0.0), axis=0, keepdims=True)
    wide = jnp.broadcast_to(row, (count, 2 * count))
    rolled = pltpu.roll(wide, shift=count, axis=1, stride=1, stride_axis=0)
    out_ref[...] = jnp.transpose(rolled[:, :count]).astype(out_ref.dtype)


def toeplitz_build(owner, phonon, count):
    return pl.pallas_call(
        toeplitz_build_kernel,
        out_shape=jax.ShapeDtypeStruct((count, count), jnp.bfloat16),
        in_specs=[pl.BlockSpec(memory_space=pltpu.SMEM), pl.BlockSpec(memory_space=pltpu.VMEM)],
        out_specs=pl.BlockSpec(memory_space=pltpu.VMEM),
        cost_estimate=pl.CostEstimate(
            flops=0, bytes_accessed=2 * (phonon.size + count * count), transcendentals=0
        ),
    )(owner, phonon)


def toeplitz_kernel(kernel_ref, packed_ref, out_ref, blocks_ref):
    peers, energies, comps = blocks_ref.shape
    count = peers * energies
    load_packed(packed_ref, blocks_ref)
    product = jnp.dot(
        kernel_ref[...], blocks_ref[...].reshape(count, comps), preferred_element_type=jnp.float32
    )
    store_packed(out_ref, product.astype(out_ref.dtype).reshape(peers, energies, comps))


def toeplitz_apply(kernel_t, packed, energies):
    peers = packed.shape[0]
    comps = packed.shape[2] * 2 // energies
    count = peers * energies
    vmem = pl.BlockSpec(memory_space=pltpu.VMEM)
    return pl.pallas_call(
        toeplitz_kernel,
        out_shape=jax.ShapeDtypeStruct(packed.shape, jnp.bfloat16),
        in_specs=[vmem, vmem],
        out_specs=vmem,
        scratch_shapes=[pltpu.VMEM((peers, energies, comps), jnp.bfloat16)],
        cost_estimate=pl.CostEstimate(
            flops=2 * count * count * comps,
            bytes_accessed=2 * (count * count + 2 * count * comps),
            transcendentals=0,
        ),
    )(kernel_t, packed)


def neighbour_kernel(neighbours_ref, low_ref, green_ref, high_ref, superop_ref, out_ref, rows_ref, picked_ref):
    width = low_ref.shape[1]
    atoms, energies, comps = green_ref.shape
    slots = superop_ref.shape[0]
    first = lax.axis_index("atoms") * atoms - width
    empty = 2 * width + atoms
    rows_ref[width:width + atoms] = green_ref[...]
    for atom in range(width):
        rows_ref[atom] = low_ref[:, atom, :]
        rows_ref[width + atoms + atom] = high_ref[:, atom, :]
    rows_ref[2 * width + atoms] = jnp.zeros((energies, comps), rows_ref.dtype)

    def pick(atom, carry):
        for slot in range(slots):
            target = neighbours_ref[slot, atom]
            row = jnp.where(target >= 0, target - first, empty)
            picked_ref[slot, atom] = rows_ref[row]
        return carry

    lax.fori_loop(0, atoms, pick, 0, unroll=True)
    total = jnp.zeros((atoms * energies, comps), jnp.float32)
    for slot in range(slots):
        total = total + jnp.dot(
            picked_ref[slot].reshape(atoms * energies, comps),
            superop_ref[slot],
            preferred_element_type=jnp.float32,
        )
    store_packed(out_ref, total.astype(out_ref.dtype).reshape(atoms, energies, comps))


def neighbour_apply(neighbours, low, green_t, high, superop):
    width = low.shape[1]
    atoms, energies, comps = green_t.shape
    slots = superop.shape[0]
    vmem = pl.BlockSpec(memory_space=pltpu.VMEM)
    return pl.pallas_call(
        neighbour_kernel,
        out_shape=jax.ShapeDtypeStruct((atoms, 2, energies * comps // 2), jnp.bfloat16),
        in_specs=[pl.BlockSpec(memory_space=pltpu.SMEM)] + [vmem] * 4,
        out_specs=vmem,
        scratch_shapes=[
            pltpu.VMEM((2 * width + atoms + 1, energies, comps), jnp.bfloat16),
            pltpu.VMEM((slots, atoms, energies, comps), jnp.bfloat16),
        ],
        cost_estimate=pl.CostEstimate(
            flops=2 * slots * atoms * energies * comps * comps,
            bytes_accessed=2 * (2 * low.size + 2 * green_t.size + superop.size),
            transcendentals=0,
        ),
    )(neighbours, low, green_t, high, superop)


def per_device(green, superop, phonon, owner, neighbours):
    local_energies = green.shape[0]
    group_size = green.shape[1]
    comps = green.shape[2]
    groups = lax.axis_size("atoms")
    green_t = jnp.transpose(green, (1, 0, 2))
    forward = [(i, i + 1) for i in range(groups - 1)]
    backward = [(i + 1, i) for i in range(groups - 1)]
    low = lax.ppermute(green[:, group_size - EDGE:], "atoms", forward)
    high = lax.ppermute(green[:, :EDGE], "atoms", backward)
    outgoing = neighbour_apply(neighbours.T, low, green_t, high, superop)
    count = local_energies * lax.axis_size("energy")
    kernel_t = toeplitz_build(owner.T, phonon, count)
    columns = lax.all_to_all(outgoing, "energy", split_axis=0, concat_axis=0, tiled=True)
    product = toeplitz_apply(kernel_t, columns, local_energies)
    result = lax.all_to_all(product, "energy", split_axis=0, concat_axis=0, tiled=True)
    result = result.reshape(result.shape[0], local_energies, comps)
    return jnp.transpose(result, (1, 0, 2))


def solution(mesh):
    return jax.shard_map(
        per_device,
        mesh=mesh,
        in_specs=(P("energy", "atoms", None), P(), P(), P("atoms", None), P("atoms", None)),
        out_specs=P("energy", "atoms", None),
        check_vma=False,
    )
```

```python
import jax
import jax.numpy as jnp
from jax import lax
from jax.experimental import pallas as pl
from jax.experimental.pallas import tpu as pltpu
from jax.sharding import PartitionSpec as P

HALO = 8
EDGE = 8
PACK = 16
ATOMS_DEV = 1


def store_packed(out_ref, blocks):
    energies, comps = blocks.shape[1], blocks.shape[2]
    half = energies // 2
    for h in range(2):
        for e in range(half):
            out_ref[:, h, e * comps:(e + 1) * comps] = blocks[:, h * half + e, :]


def load_packed(packed_ref, blocks_ref):
    energies, comps = blocks_ref.shape[1], blocks_ref.shape[2]
    half = energies // 2
    for h in range(2):
        for e in range(half):
            blocks_ref[:, h * half + e, :] = packed_ref[:, h, e * comps:(e + 1) * comps]


def toeplitz_build_kernel(owner_ref, phonon_ref, out_ref):
    count = out_ref.shape[0]
    domain = owner_ref[0, lax.axis_index("energy")]
    base = pl.multiple_of((domain // 16) * 16, 16)
    block = phonon_ref[pl.ds(base, 16), :].astype(jnp.float32)
    rows = lax.broadcasted_iota(jnp.int32, block.shape, 0)
    row = jnp.sum(jnp.where(rows == domain - base, block, 0.0), axis=0, keepdims=True)
    wide = jnp.broadcast_to(row, (count, 2 * count))
    rolled = pltpu.roll(wide, shift=count, axis=1, stride=1, stride_axis=0)
    kernel = jnp.transpose(rolled[:, :count]).astype(jnp.bfloat16)
    peers = count // PACK
    place = lax.broadcasted_iota(jnp.int32, (count, count), 0)
    energy = lax.broadcasted_iota(jnp.int32, (count, count), 1)
    order = (energy == PACK * (place % peers) + place // peers).astype(jnp.bfloat16)
    rows_first = jnp.dot(order, kernel, preferred_element_type=jnp.float32).astype(jnp.bfloat16)
    out_ref[...] = lax.dot_general(
        rows_first, order, (((1,), (1,)), ((), ())), preferred_element_type=jnp.float32
    ).astype(out_ref.dtype)


def toeplitz_build(owner, phonon, count):
    return pl.pallas_call(
        toeplitz_build_kernel,
        out_shape=jax.ShapeDtypeStruct((count, count), jnp.bfloat16),
        in_specs=[pl.BlockSpec(memory_space=pltpu.SMEM), pl.BlockSpec(memory_space=pltpu.VMEM)],
        out_specs=pl.BlockSpec(memory_space=pltpu.VMEM),
        cost_estimate=pl.CostEstimate(
            flops=0, bytes_accessed=2 * (phonon.size + count * count), transcendentals=0
        ),
    )(owner, phonon)


def toeplitz_kernel(kernel_ref, packed_ref, out_ref, columns_ref):
    peers = packed_ref.shape[0]
    comps = columns_ref.shape[1]
    half = packed_ref.shape[2] // comps
    for h in range(2):
        for e in range(half):
            block = (h * half + e) * peers
            columns_ref[block:block + peers, :] = packed_ref[:, h, e * comps:(e + 1) * comps]
    product = jnp.dot(kernel_ref[...], columns_ref[...], preferred_element_type=jnp.float32)
    product = product.astype(out_ref.dtype)
    for h in range(2):
        for e in range(half):
            block = (h * half + e) * peers
            out_ref[:, h, e * comps:(e + 1) * comps] = product[block:block + peers, :]


def toeplitz_apply(kernel_t, packed, energies):
    peers = packed.shape[0]
    comps = packed.shape[2] * 2 // energies
    count = peers * energies
    vmem = pl.BlockSpec(memory_space=pltpu.VMEM)
    return pl.pallas_call(
        toeplitz_kernel,
        out_shape=jax.ShapeDtypeStruct(packed.shape, jnp.bfloat16),
        in_specs=[vmem, vmem],
        out_specs=vmem,
        scratch_shapes=[pltpu.VMEM((count, comps), jnp.bfloat16)],
        cost_estimate=pl.CostEstimate(
            flops=2 * count * count * comps,
            bytes_accessed=2 * (count * count + 2 * count * comps),
            transcendentals=0,
        ),
    )(kernel_t, packed)


def neighbour_kernel(neighbours_ref, low_ref, green_ref, high_ref, superop_ref, out_ref, rows_ref, picked_ref):
    width = low_ref.shape[1]
    atoms, energies, comps = green_ref.shape
    slots = superop_ref.shape[0]
    first = lax.axis_index("atoms") * atoms - width
    empty = 2 * width + atoms
    rows_ref[width:width + atoms] = green_ref[...]
    for atom in range(width):
        rows_ref[atom] = low_ref[:, atom, :]
        rows_ref[width + atoms + atom] = high_ref[:, atom, :]
    rows_ref[2 * width + atoms] = jnp.zeros((energies, comps), rows_ref.dtype)

    def pick(atom, carry):
        for slot in range(slots):
            target = neighbours_ref[slot, atom]
            row = jnp.where(target >= 0, target - first, empty)
            picked_ref[slot, atom] = rows_ref[row]
        return carry

    lax.fori_loop(0, atoms, pick, 0, unroll=True)
    total = jnp.zeros((atoms * energies, comps), jnp.float32)
    for slot in range(slots):
        total = total + jnp.dot(
            picked_ref[slot].reshape(atoms * energies, comps),
            superop_ref[slot],
            preferred_element_type=jnp.float32,
        )
    store_packed(out_ref, total.astype(out_ref.dtype).reshape(atoms, energies, comps))


def neighbour_apply(neighbours, low, green_t, high, superop):
    width = low.shape[1]
    atoms, energies, comps = green_t.shape
    slots = superop.shape[0]
    vmem = pl.BlockSpec(memory_space=pltpu.VMEM)
    return pl.pallas_call(
        neighbour_kernel,
        out_shape=jax.ShapeDtypeStruct((atoms, 2, energies * comps // 2), jnp.bfloat16),
        in_specs=[pl.BlockSpec(memory_space=pltpu.SMEM)] + [vmem] * 4,
        out_specs=vmem,
        scratch_shapes=[
            pltpu.VMEM((2 * width + atoms + 1, energies, comps), jnp.bfloat16),
            pltpu.VMEM((slots, atoms, energies, comps), jnp.bfloat16),
        ],
        cost_estimate=pl.CostEstimate(
            flops=2 * slots * atoms * energies * comps * comps,
            bytes_accessed=2 * (2 * low.size + 2 * green_t.size + superop.size),
            transcendentals=0,
        ),
    )(neighbours, low, green_t, high, superop)


def per_device(green, superop, phonon, owner, neighbours):
    local_energies = green.shape[0]
    group_size = green.shape[1]
    comps = green.shape[2]
    groups = lax.axis_size("atoms")
    green_t = jnp.transpose(green, (1, 0, 2))
    forward = [(i, i + 1) for i in range(groups - 1)]
    backward = [(i + 1, i) for i in range(groups - 1)]
    low = lax.ppermute(green[:, group_size - EDGE:], "atoms", forward)
    high = lax.ppermute(green[:, :EDGE], "atoms", backward)
    outgoing = neighbour_apply(neighbours.T, low, green_t, high, superop)
    count = local_energies * lax.axis_size("energy")
    kernel_t = toeplitz_build(owner.T, phonon, count)
    columns = lax.all_to_all(outgoing, "energy", split_axis=0, concat_axis=0, tiled=True)
    product = toeplitz_apply(kernel_t, columns, local_energies)
    result = lax.all_to_all(product, "energy", split_axis=0, concat_axis=0, tiled=True)
    result = result.reshape(result.shape[0], local_energies, comps)
    return jnp.transpose(result, (1, 0, 2))


def solution(mesh):
    return jax.shard_map(
        per_device,
        mesh=mesh,
        in_specs=(P("energy", "atoms", None), P(), P(), P("atoms", None), P("atoms", None)),
        out_specs=P("energy", "atoms", None),
        check_vma=False,
    )
```

```python
import jax
import jax.numpy as jnp
from jax import lax
from jax.experimental import pallas as pl
from jax.experimental.pallas import tpu as pltpu
from jax.sharding import PartitionSpec as P

HALO = 8
EDGE = 8
ATOMS_DEV = 1


def store_packed(out_ref, blocks):
    energies, comps = blocks.shape[1], blocks.shape[2]
    half = energies // 2
    for h in range(2):
        for e in range(half):
            out_ref[:, h, e * comps:(e + 1) * comps] = blocks[:, h * half + e, :]


def load_packed(packed_ref, blocks_ref):
    energies, comps = blocks_ref.shape[1], blocks_ref.shape[2]
    half = energies // 2
    for h in range(2):
        for e in range(half):
            blocks_ref[:, h * half + e, :] = packed_ref[:, h, e * comps:(e + 1) * comps]


def toeplitz_kernel(owner_ref, phonon_ref, packed_ref, out_ref, blocks_ref):
    peers, energies, comps = blocks_ref.shape
    count = peers * energies
    load_packed(packed_ref, blocks_ref)
    domain = owner_ref[0, lax.axis_index("energy")]
    base = pl.multiple_of((domain // 16) * 16, 16)
    block = phonon_ref[pl.ds(base, 16), :].astype(jnp.float32)
    rows = lax.broadcasted_iota(jnp.int32, block.shape, 0)
    row = jnp.sum(jnp.where(rows == domain - base, block, 0.0), axis=0, keepdims=True)
    wide = jnp.broadcast_to(row, (count, 2 * count))
    rolled = pltpu.roll(wide, shift=count, axis=1, stride=1, stride_axis=0)
    kernel = jnp.transpose(rolled[:, :count]).astype(jnp.bfloat16)
    product = jnp.dot(
        kernel, blocks_ref[...].reshape(count, comps), preferred_element_type=jnp.float32
    )
    store_packed(out_ref, product.astype(out_ref.dtype).reshape(peers, energies, comps))


def toeplitz_apply(owner, phonon, packed, energies):
    peers = packed.shape[0]
    comps = packed.shape[2] * 2 // energies
    count = peers * energies
    vmem = pl.BlockSpec(memory_space=pltpu.VMEM)
    return pl.pallas_call(
        toeplitz_kernel,
        out_shape=jax.ShapeDtypeStruct(packed.shape, jnp.bfloat16),
        in_specs=[pl.BlockSpec(memory_space=pltpu.SMEM), vmem, vmem],
        out_specs=vmem,
        scratch_shapes=[pltpu.VMEM((peers, energies, comps), jnp.bfloat16)],
        cost_estimate=pl.CostEstimate(
            flops=2 * count * count * comps,
            bytes_accessed=2 * (phonon.size + 2 * count * comps),
            transcendentals=0,
        ),
    )(owner, phonon, packed)


def neighbour_kernel(neighbours_ref, low_ref, green_ref, high_ref, superop_ref, out_ref, rows_ref, picked_ref):
    width = low_ref.shape[1]
    atoms, energies, comps = green_ref.shape
    slots = superop_ref.shape[0]
    first = lax.axis_index("atoms") * atoms - width
    empty = 2 * width + atoms
    rows_ref[width:width + atoms] = green_ref[...]
    for atom in range(width):
        rows_ref[atom] = low_ref[:, atom, :]
        rows_ref[width + atoms + atom] = high_ref[:, atom, :]
    rows_ref[2 * width + atoms] = jnp.zeros((energies, comps), rows_ref.dtype)

    def pick(atom, carry):
        for slot in range(slots):
            target = neighbours_ref[slot, atom]
            row = jnp.where(target >= 0, target - first, empty)
            picked_ref[slot, atom] = rows_ref[row]
        return carry

    lax.fori_loop(0, atoms, pick, 0, unroll=True)
    total = jnp.zeros((atoms * energies, comps), jnp.float32)
    for slot in range(slots):
        total = total + jnp.dot(
            picked_ref[slot].reshape(atoms * energies, comps),
            superop_ref[slot],
            preferred_element_type=jnp.float32,
        )
    store_packed(out_ref, total.astype(out_ref.dtype).reshape(atoms, energies, comps))


def neighbour_apply(neighbours, low, green_t, high, superop):
    width = low.shape[1]
    atoms, energies, comps = green_t.shape
    slots = superop.shape[0]
    vmem = pl.BlockSpec(memory_space=pltpu.VMEM)
    return pl.pallas_call(
        neighbour_kernel,
        out_shape=jax.ShapeDtypeStruct((atoms, 2, energies * comps // 2), jnp.bfloat16),
        in_specs=[pl.BlockSpec(memory_space=pltpu.SMEM)] + [vmem] * 4,
        out_specs=vmem,
        scratch_shapes=[
            pltpu.VMEM((2 * width + atoms + 1, energies, comps), jnp.bfloat16),
            pltpu.VMEM((slots, atoms, energies, comps), jnp.bfloat16),
        ],
        cost_estimate=pl.CostEstimate(
            flops=2 * slots * atoms * energies * comps * comps,
            bytes_accessed=2 * (2 * low.size + 2 * green_t.size + superop.size),
            transcendentals=0,
        ),
    )(neighbours, low, green_t, high, superop)


def per_device(green, superop, phonon, owner, neighbours):
    local_energies = green.shape[0]
    group_size = green.shape[1]
    comps = green.shape[2]
    groups = lax.axis_size("atoms")
    green_t = jnp.transpose(green, (1, 0, 2))
    forward = [(i, i + 1) for i in range(groups - 1)]
    backward = [(i + 1, i) for i in range(groups - 1)]
    low = lax.ppermute(green[:, group_size - EDGE:], "atoms", forward)
    high = lax.ppermute(green[:, :EDGE], "atoms", backward)
    outgoing = neighbour_apply(neighbours.T, low, green_t, high, superop)
    owner_t, outgoing = lax.optimization_barrier((owner.T, outgoing))
    columns = lax.all_to_all(outgoing, "energy", split_axis=0, concat_axis=0, tiled=True)
    product = toeplitz_apply(owner_t, phonon, columns, local_energies)
    result = lax.all_to_all(product, "energy", split_axis=0, concat_axis=0, tiled=True)
    result = result.reshape(result.shape[0], local_energies, comps)
    return jnp.transpose(result, (1, 0, 2))


def solution(mesh):
    return jax.shard_map(
        per_device,
        mesh=mesh,
        in_specs=(P("energy", "atoms", None), P(), P(), P("atoms", None), P("atoms", None)),
        out_specs=P("energy", "atoms", None),
        check_vma=False,
    )
```

```python
import jax
import jax.numpy as jnp
from jax import lax
from jax.experimental import pallas as pl
from jax.experimental.pallas import tpu as pltpu
from jax.sharding import PartitionSpec as P

HALO = 8
EDGE = 8
ATOMS_DEV = 1


def store_packed(out_ref, blocks):
    energies, comps = blocks.shape[1], blocks.shape[2]
    half = energies // 2
    for h in range(2):
        for e in range(half):
            out_ref[:, h, e * comps:(e + 1) * comps] = blocks[:, h * half + e, :]


def load_packed(packed_ref, blocks_ref):
    energies, comps = blocks_ref.shape[1], blocks_ref.shape[2]
    half = energies // 2
    for h in range(2):
        for e in range(half):
            blocks_ref[:, h * half + e, :] = packed_ref[:, h, e * comps:(e + 1) * comps]


def toeplitz_kernel(owner_ref, phonon_ref, packed_ref, out_ref, blocks_ref):
    peers, energies, comps = blocks_ref.shape
    count = peers * energies
    load_packed(packed_ref, blocks_ref)
    domain = owner_ref[0, lax.axis_index("energy")]
    base = pl.multiple_of((domain // 16) * 16, 16)
    block = phonon_ref[pl.ds(base, 16), :].astype(jnp.float32)
    rows = lax.broadcasted_iota(jnp.int32, block.shape, 0)
    row = jnp.sum(jnp.where(rows == domain - base, block, 0.0), axis=0, keepdims=True)
    wide = jnp.broadcast_to(row.astype(jnp.bfloat16), (count, 2 * count))
    rolled = pltpu.roll(wide, shift=count, axis=1, stride=1, stride_axis=0)
    kernel = jnp.transpose(rolled[:, :count])
    product = jnp.dot(
        kernel, blocks_ref[...].reshape(count, comps), preferred_element_type=jnp.float32
    )
    store_packed(out_ref, product.astype(out_ref.dtype).reshape(peers, energies, comps))


def toeplitz_apply(owner, phonon, packed, energies):
    peers = packed.shape[0]
    comps = packed.shape[2] * 2 // energies
    count = peers * energies
    vmem = pl.BlockSpec(memory_space=pltpu.VMEM)
    return pl.pallas_call(
        toeplitz_kernel,
        out_shape=jax.ShapeDtypeStruct(packed.shape, jnp.bfloat16),
        in_specs=[pl.BlockSpec(memory_space=pltpu.SMEM), vmem, vmem],
        out_specs=vmem,
        scratch_shapes=[pltpu.VMEM((peers, energies, comps), jnp.bfloat16)],
        cost_estimate=pl.CostEstimate(
            flops=2 * count * count * comps,
            bytes_accessed=2 * (phonon.size + 2 * count * comps),
            transcendentals=0,
        ),
    )(owner, phonon, packed)


def neighbour_kernel(neighbours_ref, low_ref, green_ref, high_ref, superop_ref, out_ref, rows_ref, picked_ref):
    width = low_ref.shape[1]
    atoms, energies, comps = green_ref.shape
    slots = superop_ref.shape[0]
    first = lax.axis_index("atoms") * atoms - width
    empty = 2 * width + atoms
    rows_ref[width:width + atoms] = green_ref[...]
    for atom in range(width):
        rows_ref[atom] = low_ref[:, atom, :]
        rows_ref[width + atoms + atom] = high_ref[:, atom, :]
    rows_ref[2 * width + atoms] = jnp.zeros((energies, comps), rows_ref.dtype)

    def pick(atom, carry):
        for slot in range(slots):
            target = neighbours_ref[slot, atom]
            row = jnp.where(target >= 0, target - first, empty)
            picked_ref[slot, atom] = rows_ref[row]
        return carry

    lax.fori_loop(0, atoms, pick, 0, unroll=True)
    total = jnp.zeros((atoms * energies, comps), jnp.float32)
    for slot in range(slots):
        total = total + jnp.dot(
            picked_ref[slot].reshape(atoms * energies, comps),
            superop_ref[slot],
            preferred_element_type=jnp.float32,
        )
    store_packed(out_ref, total.astype(out_ref.dtype).reshape(atoms, energies, comps))


def neighbour_apply(neighbours, low, green_t, high, superop):
    width = low.shape[1]
    atoms, energies, comps = green_t.shape
    slots = superop.shape[0]
    vmem = pl.BlockSpec(memory_space=pltpu.VMEM)
    return pl.pallas_call(
        neighbour_kernel,
        out_shape=jax.ShapeDtypeStruct((atoms, 2, energies * comps // 2), jnp.bfloat16),
        in_specs=[pl.BlockSpec(memory_space=pltpu.SMEM)] + [vmem] * 4,
        out_specs=vmem,
        scratch_shapes=[
            pltpu.VMEM((2 * width + atoms + 1, energies, comps), jnp.bfloat16),
            pltpu.VMEM((slots, atoms, energies, comps), jnp.bfloat16),
        ],
        cost_estimate=pl.CostEstimate(
            flops=2 * slots * atoms * energies * comps * comps,
            bytes_accessed=2 * (2 * low.size + 2 * green_t.size + superop.size),
            transcendentals=0,
        ),
    )(neighbours, low, green_t, high, superop)


def per_device(green, superop, phonon, owner, neighbours):
    local_energies = green.shape[0]
    group_size = green.shape[1]
    comps = green.shape[2]
    groups = lax.axis_size("atoms")
    green_t = jnp.transpose(green, (1, 0, 2))
    forward = [(i, i + 1) for i in range(groups - 1)]
    backward = [(i + 1, i) for i in range(groups - 1)]
    low = lax.ppermute(green[:, group_size - EDGE:], "atoms", forward)
    high = lax.ppermute(green[:, :EDGE], "atoms", backward)
    outgoing = neighbour_apply(neighbours.T, low, green_t, high, superop)
    owner_t, outgoing = lax.optimization_barrier((owner.T, outgoing))
    columns = lax.all_to_all(outgoing, "energy", split_axis=0, concat_axis=0, tiled=True)
    product = toeplitz_apply(owner_t, phonon, columns, local_energies)
    result = lax.all_to_all(product, "energy", split_axis=0, concat_axis=0, tiled=True)
    result = result.reshape(result.shape[0], local_energies, comps)
    return jnp.transpose(result, (1, 0, 2))


def solution(mesh):
    return jax.shard_map(
        per_device,
        mesh=mesh,
        in_specs=(P("energy", "atoms", None), P(), P(), P("atoms", None), P("atoms", None)),
        out_specs=P("energy", "atoms", None),
        check_vma=False,
    )
```

```python
import jax
import jax.numpy as jnp
from jax import lax
from jax.experimental import pallas as pl
from jax.experimental.pallas import tpu as pltpu
from jax.sharding import PartitionSpec as P

HALO = 8
EDGE = 8
ATOMS_DEV = 1


def store_packed(out_ref, blocks):
    energies, comps = blocks.shape[1], blocks.shape[2]
    half = energies // 2
    for h in range(2):
        for e in range(half):
            out_ref[:, h, e * comps:(e + 1) * comps] = blocks[:, h * half + e, :]


def load_packed(packed_ref, blocks_ref):
    energies, comps = blocks_ref.shape[1], blocks_ref.shape[2]
    half = energies // 2
    for h in range(2):
        for e in range(half):
            blocks_ref[:, h * half + e, :] = packed_ref[:, h, e * comps:(e + 1) * comps]


def toeplitz_kernel(owner_ref, phonon_ref, packed_ref, out_ref, blocks_ref):
    peers, energies, comps = blocks_ref.shape
    count = peers * energies
    load_packed(packed_ref, blocks_ref)
    domain = owner_ref[0, lax.axis_index("energy")]
    base = pl.multiple_of((domain // 16) * 16, 16)
    block = phonon_ref[pl.ds(base, 16), :].astype(jnp.float32)
    rows = lax.broadcasted_iota(jnp.int32, block.shape, 0)
    row = jnp.sum(jnp.where(rows == domain - base, block, 0.0), axis=0, keepdims=True)
    wide = jnp.broadcast_to(row.astype(jnp.bfloat16), (count, 2 * count))
    rolled = pltpu.roll(wide, shift=count, axis=1, stride=1, stride_axis=0)
    kernel = jnp.transpose(rolled[:, :count])
    product = jnp.dot(
        kernel, blocks_ref[...].reshape(count, comps), preferred_element_type=jnp.float32
    )
    store_packed(out_ref, product.astype(out_ref.dtype).reshape(peers, energies, comps))


def toeplitz_apply(owner, phonon, packed, energies):
    peers = packed.shape[0]
    comps = packed.shape[2] * 2 // energies
    count = peers * energies
    vmem = pl.BlockSpec(memory_space=pltpu.VMEM)
    return pl.pallas_call(
        toeplitz_kernel,
        out_shape=jax.ShapeDtypeStruct(packed.shape, jnp.bfloat16),
        in_specs=[pl.BlockSpec(memory_space=pltpu.SMEM), vmem, vmem],
        out_specs=vmem,
        scratch_shapes=[pltpu.VMEM((peers, energies, comps), jnp.bfloat16)],
        cost_estimate=pl.CostEstimate(
            flops=2 * count * count * comps,
            bytes_accessed=2 * (phonon.size + 2 * count * comps),
            transcendentals=0,
        ),
    )(owner, phonon, packed)


def neighbour_kernel(neighbours_ref, low_ref, green_ref, high_ref, superop_ref, out_ref, rows_ref, picked_ref):
    width = low_ref.shape[1]
    atoms, energies, comps = green_ref.shape
    slots = superop_ref.shape[0]
    first = lax.axis_index("atoms") * atoms - width
    empty = 2 * width + atoms
    rows_ref[width:width + atoms] = green_ref[...]
    for atom in range(width):
        rows_ref[atom] = low_ref[:, atom, :]
        rows_ref[width + atoms + atom] = high_ref[:, atom, :]
    rows_ref[2 * width + atoms] = jnp.zeros((energies, comps), rows_ref.dtype)

    def pick(atom, carry):
        for slot in range(slots):
            target = neighbours_ref[slot, atom]
            row = jnp.where(target >= 0, target - first, empty)
            picked_ref[slot, atom] = rows_ref[row]
        return carry

    lax.fori_loop(0, atoms, pick, 0, unroll=True)
    total = jnp.zeros((atoms * energies, comps), jnp.float32)
    for slot in range(slots):
        total = total + jnp.dot(
            picked_ref[slot].reshape(atoms * energies, comps),
            superop_ref[slot],
            preferred_element_type=jnp.float32,
        )
    store_packed(out_ref, total.astype(out_ref.dtype).reshape(atoms, energies, comps))


def neighbour_apply(neighbours, low, green_t, high, superop):
    width = low.shape[1]
    atoms, energies, comps = green_t.shape
    slots = superop.shape[0]
    vmem = pl.BlockSpec(memory_space=pltpu.VMEM)
    return pl.pallas_call(
        neighbour_kernel,
        out_shape=jax.ShapeDtypeStruct((atoms, 2, energies * comps // 2), jnp.bfloat16),
        in_specs=[pl.BlockSpec(memory_space=pltpu.SMEM)] + [vmem] * 4,
        out_specs=vmem,
        scratch_shapes=[
            pltpu.VMEM((2 * width + atoms + 1, energies, comps), jnp.bfloat16),
            pltpu.VMEM((slots, atoms, energies, comps), jnp.bfloat16),
        ],
        cost_estimate=pl.CostEstimate(
            flops=2 * slots * atoms * energies * comps * comps,
            bytes_accessed=2 * (2 * low.size + 2 * green_t.size + superop.size),
            transcendentals=0,
        ),
    )(neighbours, low, green_t, high, superop)


def per_device(green, superop, phonon, owner, neighbours):
    local_energies = green.shape[0]
    group_size = green.shape[1]
    comps = green.shape[2]
    groups = lax.axis_size("atoms")
    green_t = jnp.transpose(green, (1, 0, 2))
    forward = [(i, i + 1) for i in range(groups - 1)]
    backward = [(i + 1, i) for i in range(groups - 1)]
    low = lax.ppermute(green[:, group_size - EDGE:], "atoms", forward)
    high = lax.ppermute(green[:, :EDGE], "atoms", backward)
    outgoing = neighbour_apply(neighbours.T, low, green_t, high, superop)
    owner_t, outgoing = lax.optimization_barrier((owner.T, outgoing))
    columns = lax.all_to_all(outgoing, "energy", split_axis=0, concat_axis=0, tiled=True)
    product = toeplitz_apply(owner_t, phonon, columns, local_energies)
    result = lax.all_to_all(product, "energy", split_axis=0, concat_axis=0, tiled=True)
    result = result.reshape(result.shape[0], 2, local_energies // 2, comps)
    return jnp.transpose(result, (1, 2, 0, 3)).reshape(local_energies, result.shape[0], comps)


def solution(mesh):
    return jax.shard_map(
        per_device,
        mesh=mesh,
        in_specs=(P("energy", "atoms", None), P(), P(), P("atoms", None), P("atoms", None)),
        out_specs=P("energy", "atoms", None),
        check_vma=False,
    )
```
